256 devices in a mesh: row: 16 (over y, x), col: 16 (over z, core).
Axes of the slice: x: 4, y: 4, z: 8, core: 2. Of those that a mesh axis runs over, the one named last changes fastest.
Arguments:
- probe_block: bfloat16 [64, 262144], P(None, ('row', 'col'))
- prior_blocks: bfloat16 [4, 64, 262144], P(None, None, ('row', 'col'))
- self_relatedness: float32 [262144], P(('row', 'col')), may hold values from 0.5 to 2
- tile_values: bfloat16 [1280, 1024, 1024], P(('row', 'col')), may hold values from -0.125 to 0.125
- tile_index: int32 [1280, 3], P(('row', 'col')), may hold values from 0 to 255, as said below
Outputs:
- residual_block: float32 [64, 262144], P(None, ('row', 'col'))
- coefficients: float32 [5, 64, 64], replicated
The draws below stay inside these ranges and needn't reach their ends.
Inputs may be any that keep to these rules, and one draw needn't show every extreme that they name: `tile_index`: rows d * 5 to d * 5 + 4 belong to the device d = r * C + c at mesh position (r, c), C the size of the col axis. In a row with column 2 equal to 1 (live) the tile row lies in [r * C, r * C + C), the tile column j has j % C == c, and tile row <= tile column; live pairs of one device are distinct. Column 2 is 0 in dead rows, which repeat the indices of the device's first row. Live counts vary between devices (not all equal), and some device has all 5 rows live.
All inputs are finite; a program needn't handle non-finite values.
Results may differ from the reference program's by a relative error of at most 0.0003.
Values may be sent and summed in bfloat16 or wider, within the bound.
No kernel may reach another device: no remote copies, remote signals or barrier semaphores. Data moves between devices by JAX's collectives and lax.ppermute only.
A program may use at most 128 MiB of HBM per device.

```python
import math
import jax
import jax.numpy as jnp
from jax import lax

K = 64
TS = 1024
BLOCKS = 4
SLOTS = 5
NQ = 5
NS = 262144
N_ROW = 16
N_COL = 16


def fresh_noise(key, shape):
    return jax.random.normal(key, shape, jnp.float32)


def shared_parts(key):
    scale_key = jax.random.fold_in(key, 31)
    shared_key = jax.random.fold_in(key, 32)
    position = jnp.arange(NS, dtype=jnp.float32)
    rising = jnp.sqrt(1.0 + 2.0 * position / NS)
    spread = jnp.exp(jax.random.uniform(scale_key, (NS,), jnp.float32, math.log(0.4), math.log(4.0)))
    common = 0.6 * jax.random.normal(shared_key, (K, NS), jnp.float32)
    return (common, spread * rising)


def draw_probe_block(key, part):
    common, scales = shared_parts(key)
    own = fresh_noise(jax.random.fold_in(key, 21), (K, NS))
    return ((own + common) * scales[None, :]).astype(jnp.bfloat16)


def draw_prior_blocks(key, part):
    common, scales = shared_parts(key)
    own = fresh_noise(jax.random.fold_in(key, 22), (BLOCKS, K, NS))
    return ((own + common[None]) * scales[None, None, :]).astype(jnp.bfloat16)


def draw_tile_index(key, part):
    devices = N_ROW * N_COL
    device = jnp.arange(devices, dtype=jnp.int32)[:, None]
    candidate = jnp.arange(devices, dtype=jnp.int32)[None, :]
    row_block = device // N_COL
    col_set = device % N_COL
    tile_row = row_block * N_COL + candidate // N_ROW
    tile_col = candidate % N_ROW * N_COL + col_set
    allowed = tile_row <= tile_col
    scores = jax.random.randint(jax.random.fold_in(key, 41), (devices, devices), 0, 1 << 20) * devices + candidate
    ranked = jnp.where(allowed, scores, (1 << 30) + candidate)
    order = jnp.argsort(ranked, axis=1)[:, :SLOTS]
    picked_row = jnp.take_along_axis(jnp.broadcast_to(tile_row, (devices, devices)), order, axis=1)
    picked_col = jnp.take_along_axis(jnp.broadcast_to(tile_col, (devices, devices)), order, axis=1)
    available = jnp.sum(allowed.astype(jnp.int32), axis=1)
    first_draw = jax.random.randint(jax.random.fold_in(key, 42), (devices,), 0, SLOTS)
    second_draw = jax.random.randint(jax.random.fold_in(key, 43), (devices,), 0, SLOTS)
    wanted = 1 + jnp.minimum(first_draw, second_draw)
    full_device = jax.random.randint(jax.random.fold_in(key, 44), (), 0, N_COL)
    wanted = jnp.where(jnp.arange(devices, dtype=jnp.int32) == full_device, SLOTS, wanted)
    active_count = jnp.minimum(wanted, available)
    slot_number = jnp.arange(SLOTS, dtype=jnp.int32)[None, :]
    active = slot_number < active_count[:, None]
    rows_out = jnp.where(active, picked_row, picked_row[:, :1])
    cols_out = jnp.where(active, picked_col, picked_col[:, :1])
    flags = active.astype(jnp.int32)
    table = jnp.stack([rows_out, cols_out, flags], axis=-1)
    return table.reshape(devices * SLOTS, 3).astype(jnp.int32)


def steps_of(key, shape, shards, smallest, high):
    level = 1.0
    for dim, blocks in shards:
        draws = jax.random.uniform(jax.random.fold_in(jax.random.fold_in(key, 6), dim), (blocks,), jnp.float32, smallest / len(shards), high / len(shards))
        level = level * jnp.repeat(jnp.exp(draws), shape[dim] // blocks).reshape((-1,) + (1,) * (len(shape) - 1 - dim))
    return level


def bell_draw(stream_key, extent, scale, most, shards=(), kind=jnp.bfloat16):
    entries = jax.random.normal(stream_key, extent, jnp.float32) * scale
    if len(shards) > 0:
        entries = steps_of(stream_key, extent, shards, -0.22, 0.18) * entries
    return jnp.clip(entries, min=-most, max=most).astype(kind)


def setup_inputs(seed: int = 0) -> dict:
    key_of = jax.random.split(jax.random.key(seed), 6)
    return {
        "probe_block": draw_probe_block(jax.random.fold_in(key_of[5], 71), 0),
        "prior_blocks": draw_prior_blocks(jax.random.fold_in(key_of[5], 71), 0),
        "self_relatedness": jnp.clip(jnp.exp(math.log(2.0) - 1.3862944 * jax.random.uniform(key_of[2], (NS,), jnp.float32) ** steps_of(key_of[2], (NS,), ((0, 256),), -0.2, 0.2)), 0.5, 2.0),
        "tile_values": bell_draw(key_of[3], (N_ROW * N_COL * SLOTS, TS, TS), (2 * TS) ** -0.5, 0.125, ((0, 256),)),
        "tile_index": draw_tile_index(jax.random.fold_in(key_of[5], 71), 0),
    }


def add_span(running, addend, offset):
    current = lax.dynamic_slice_in_dim(running, offset, addend.shape[1], 1)
    return lax.dynamic_update_slice_in_dim(running, current + addend, offset, 1)

def keep_same(running):
    return running

def reference(probe_block, prior_blocks, self_relatedness, tile_values, tile_index):
    tile_width = tile_values.shape[1]
    start = self_relatedness[None, :] * probe_block.astype(jnp.float32)

    def accumulate(running, inputs):
        current_tile, entry = inputs

        def apply(state):
            row_start = (entry[0] * tile_width).astype(jnp.int32)
            col_start = (entry[1] * tile_width).astype(jnp.int32)
            right = lax.dynamic_slice_in_dim(probe_block, col_start, tile_width, 1)
            left = lax.dynamic_slice_in_dim(probe_block, row_start, tile_width, 1)
            forward = lax.dot_general(right.astype(jnp.float32), current_tile.astype(jnp.float32), (((1,), (1,)), ((), ())), preferred_element_type=jnp.float32)
            mirror = jnp.dot(left.astype(jnp.float32), current_tile.astype(jnp.float32), preferred_element_type=jnp.float32)
            state = add_span(state, forward, row_start)
            return add_span(state, mirror, col_start)
        return (lax.cond(entry[2] > 0, apply, keep_same, running), None)
    product, _ = lax.scan(accumulate, start, (tile_values, tile_index))
    basis = jnp.concatenate([prior_blocks, probe_block[None]], axis=0)
    current = product
    solved = []
    for block_number in range(NQ):
        basis_block = basis[block_number]
        gram_block = jnp.dot(basis_block.astype(jnp.float32), basis_block.T.astype(jnp.float32), preferred_element_type=jnp.float32)
        wide_block = basis_block.astype(jnp.float32)
        along = jnp.dot(wide_block, current.T, precision=lax.Precision.HIGHEST)
        factor = jnp.linalg.cholesky(gram_block)
        coefficient = jax.scipy.linalg.cho_solve((factor, True), along)
        solved.append(coefficient)
        current = current - jnp.dot(coefficient.T, wide_block, precision=lax.Precision.HIGHEST)
    return (current, jnp.stack(solved))
```

```python
import jax
import jax.numpy as jnp
from jax import lax
from jax.sharding import PartitionSpec as P


def add_span(running, addend, offset):
    current = lax.dynamic_slice_in_dim(running, offset, addend.shape[1], 1)
    return lax.dynamic_update_slice_in_dim(running, current + addend, offset, 1)


def keep_same(partials):
    return partials


def tile_products(tile_values, tile_index, row_probes, col_probes, col_count):
    tile_width = tile_values.shape[1]
    depth = row_probes.shape[0]
    partials = []
    partials.append(jnp.zeros((depth, row_probes.shape[1]), jnp.float32))
    partials.append(jnp.zeros((depth, col_probes.shape[1]), jnp.float32))
    partials = tuple(partials)
    for slot_index in range(tile_values.shape[0]):
        current_tile = tile_values[slot_index]
        row_start = tile_index[slot_index, 0] % col_count * tile_width
        col_start = tile_index[slot_index, 1] // col_count * tile_width

        def apply(state, current_tile=current_tile, row_start=row_start, col_start=col_start):
            updated = list(state)
            right = lax.dynamic_slice_in_dim(col_probes, col_start, tile_width, 1)
            forward = lax.dot_general(
                right, current_tile, (((1,), (1,)), ((), ())), preferred_element_type=jnp.float32
            )
            updated[0] = add_span(updated[0], forward, row_start)
            left = lax.dynamic_slice_in_dim(row_probes, row_start, tile_width, 1)
            mirror = jnp.dot(left, current_tile, preferred_element_type=jnp.float32)
            updated[1] = add_span(updated[1], mirror, col_start)
            return tuple(updated)

        partials = lax.cond(tile_index[slot_index, 2] > 0, apply, keep_same, partials)
    return partials


def sum_rows(row_part):
    return lax.psum_scatter(row_part, "col", scatter_dimension=1, tiled=True)


def sum_columns(col_part):
    return lax.psum_scatter(col_part, "row", scatter_dimension=1, tiled=True)


def solve_block(gram_block, target):
    factor = jnp.linalg.cholesky(gram_block)
    return jax.scipy.linalg.cho_solve((factor, True), target)


def shards(probe_block, prior_blocks, self_relatedness, tile_values, tile_index):
    col_count = lax.axis_size("col")
    block_count = prior_blocks.shape[0] + 1
    depth = probe_block.shape[0]
    basis = jnp.concatenate([prior_blocks, probe_block[None]], axis=0)
    flat_basis = basis.reshape(block_count * depth, basis.shape[2])
    wide_basis = flat_basis.astype(jnp.float32)
    row_probes = lax.all_gather(probe_block, "col", axis=1, tiled=True)
    col_probes = lax.all_gather(probe_block, "row", axis=1, tiled=True)
    row_part, col_part = tile_products(tile_values, tile_index, row_probes, col_probes, col_count)
    row_total = sum_rows(row_part)
    col_total = sum_columns(col_part)
    product = self_relatedness[None, :] * probe_block.astype(jnp.float32) + row_total + col_total
    gram_local = jnp.dot(flat_basis, flat_basis.T, preferred_element_type=jnp.float32)
    along_local = jnp.dot(wide_basis, product.T, precision=lax.Precision.HIGHEST)
    gram, along = lax.psum((gram_local, along_local), ("row", "col"))
    solved = []
    for block_number in range(block_count):
        rows = slice(block_number * depth, (block_number + 1) * depth)
        target = along[rows]
        for earlier in range(block_number):
            cross = gram[rows, earlier * depth:(earlier + 1) * depth]
            target = target - jnp.dot(cross, solved[earlier], precision=lax.Precision.HIGHEST)
        solved.append(solve_block(gram[rows, rows], target))
    coefficients = jnp.concatenate(solved, axis=0)
    current = product - jnp.dot(coefficients.T, wide_basis, precision=lax.Precision.HIGHEST)
    return (current, jnp.stack(solved))


def solution(mesh):
    in_specs = (
        P(None, ("row", "col")),
        P(None, None, ("row", "col")),
        P(("row", "col")),
        P(("row", "col"), None, None),
        P(("row", "col"), None),
    )
    out_specs = (P(None, ("row", "col")), P())
    return jax.shard_map(shards, mesh=mesh, in_specs=in_specs, out_specs=out_specs, check_vma=False)
```

```python
import jax
import jax.numpy as jnp
from jax import lax
from jax.sharding import PartitionSpec as P


def add_span(running, addend, offset):
    current = lax.dynamic_slice_in_dim(running, offset, addend.shape[1], 1)
    return lax.dynamic_update_slice_in_dim(running, current + addend, offset, 1)


def keep_same(partials):
    return partials


def tile_products(tile_values, tile_index, row_probes, col_probes, col_count):
    tile_width = tile_values.shape[1]
    depth = row_probes.shape[0]
    partials = []
    partials.append(jnp.zeros((depth, row_probes.shape[1]), jnp.float32))
    partials.append(jnp.zeros((depth, col_probes.shape[1]), jnp.float32))
    partials = tuple(partials)
    for slot_index in range(tile_values.shape[0]):
        current_tile = tile_values[slot_index]
        row_start = tile_index[slot_index, 0] % col_count * tile_width
        col_start = tile_index[slot_index, 1] // col_count * tile_width

        def apply(state, current_tile=current_tile, row_start=row_start, col_start=col_start):
            updated = list(state)
            right = lax.dynamic_slice_in_dim(col_probes, col_start, tile_width, 1)
            forward = lax.dot_general(
                right, current_tile, (((1,), (1,)), ((), ())), preferred_element_type=jnp.float32
            )
            updated[0] = add_span(updated[0], forward, row_start)
            left = lax.dynamic_slice_in_dim(row_probes, row_start, tile_width, 1)
            mirror = jnp.dot(left, current_tile, preferred_element_type=jnp.float32)
            updated[1] = add_span(updated[1], mirror, col_start)
            return tuple(updated)

        partials = lax.cond(tile_index[slot_index, 2] > 0, apply, keep_same, partials)
    return partials


def sum_rows(row_part):
    return lax.psum_scatter(row_part, "col", scatter_dimension=1, tiled=True)


def sum_columns(col_part):
    return lax.psum_scatter(col_part, "row", scatter_dimension=1, tiled=True)


def hypercube_sum(value, axes):
    for axis in axes:
        size = lax.axis_size(axis)
        if size & (size - 1):
            value = lax.psum(value, axis)
            continue
        stride = 1
        while stride < size:
            pairs = [(index, index ^ stride) for index in range(size)]
            value = value + lax.ppermute(value, axis, pairs)
            stride *= 2
    return value


def inverse_factor(gram_block):
    factor = jnp.linalg.cholesky(gram_block)
    identity = jnp.eye(gram_block.shape[0], dtype=gram_block.dtype)
    return jax.scipy.linalg.solve_triangular(factor, identity, lower=True)


def shards(probe_block, prior_blocks, self_relatedness, tile_values, tile_index):
    col_count = lax.axis_size("col")
    block_count = prior_blocks.shape[0] + 1
    depth = probe_block.shape[0]
    highest = lax.Precision.HIGHEST
    basis = jnp.concatenate([prior_blocks, probe_block[None]], axis=0)
    flat_basis = basis.reshape(block_count * depth, basis.shape[2])
    wide_basis = flat_basis.astype(jnp.float32)
    gram_local = jnp.dot(flat_basis, flat_basis.T, preferred_element_type=jnp.float32)
    pairs = [(b, e) for b in range(block_count) for e in range(b + 1)]
    lower_local = jnp.stack(
        [gram_local[b * depth:(b + 1) * depth, e * depth:(e + 1) * depth] for b, e in pairs]
    )
    lower = hypercube_sum(lower_local, ("col", "row"))
    gram = {pair: lower[n] for n, pair in enumerate(pairs)}
    inverses = [inverse_factor(gram[(b, b)]) for b in range(block_count)]
    row_probes = lax.all_gather(probe_block, "col", axis=1, tiled=True)
    col_probes = lax.all_gather(probe_block, "row", axis=1, tiled=True)
    row_part, col_part = tile_products(tile_values, tile_index, row_probes, col_probes, col_count)
    row_total = sum_rows(row_part)
    col_total = sum_columns(col_part)
    product = self_relatedness[None, :] * probe_block.astype(jnp.float32) + row_total + col_total
    along_local = jnp.dot(wide_basis, product.T, precision=highest)
    along = hypercube_sum(along_local, ("col", "row"))
    solved = []
    for block_number in range(block_count):
        target = along[block_number * depth:(block_number + 1) * depth]
        for earlier in range(block_number):
            target = target - jnp.dot(gram[(block_number, earlier)], solved[earlier], precision=highest)
        inverse = inverses[block_number]
        half = jnp.dot(inverse, target, precision=highest)
        solved.append(jnp.dot(inverse.T, half, precision=highest))
    coefficients = jnp.concatenate(solved, axis=0)
    current = product - jnp.dot(coefficients.T, wide_basis, precision=highest)
    return (current, jnp.stack(solved))


def solution(mesh):
    in_specs = (
        P(None, ("row", "col")),
        P(None, None, ("row", "col")),
        P(("row", "col")),
        P(("row", "col"), None, None),
        P(("row", "col"), None),
    )
    out_specs = (P(None, ("row", "col")), P())
    return jax.shard_map(shards, mesh=mesh, in_specs=in_specs, out_specs=out_specs, check_vma=False)
```

```python
import jax
import jax.numpy as jnp
from jax import lax
from jax.sharding import PartitionSpec as P


def add_span(running, addend, offset):
    current = lax.dynamic_slice_in_dim(running, offset, addend.shape[1], 1)
    return lax.dynamic_update_slice_in_dim(running, current + addend, offset, 1)


def keep_same(partials):
    return partials


def tile_products(tile_values, tile_index, row_probes, col_probes, col_count):
    tile_width = tile_values.shape[1]
    depth = row_probes.shape[0]
    partials = []
    partials.append(jnp.zeros((depth, row_probes.shape[1]), jnp.float32))
    partials.append(jnp.zeros((depth, col_probes.shape[1]), jnp.float32))
    partials = tuple(partials)
    for slot_index in range(tile_values.shape[0]):
        current_tile = tile_values[slot_index]
        row_start = tile_index[slot_index, 0] % col_count * tile_width
        col_start = tile_index[slot_index, 1] // col_count * tile_width

        def apply(state, current_tile=current_tile, row_start=row_start, col_start=col_start):
            updated = list(state)
            right = lax.dynamic_slice_in_dim(col_probes, col_start, tile_width, 1)
            forward = lax.dot_general(
                right, current_tile, (((1,), (1,)), ((), ())), preferred_element_type=jnp.float32
            )
            updated[0] = add_span(updated[0], forward, row_start)
            left = lax.dynamic_slice_in_dim(row_probes, row_start, tile_width, 1)
            mirror = jnp.dot(left, current_tile, preferred_element_type=jnp.float32)
            updated[1] = add_span(updated[1], mirror, col_start)
            return tuple(updated)

        partials = lax.cond(tile_index[slot_index, 2] > 0, apply, keep_same, partials)
    return partials


def sum_rows(row_part):
    return lax.psum_scatter(row_part, "col", scatter_dimension=1, tiled=True)


def sum_columns(col_part):
    return lax.psum_scatter(col_part, "row", scatter_dimension=1, tiled=True)


def hypercube_sum(value, axes):
    for axis in axes:
        size = lax.axis_size(axis)
        if size & (size - 1):
            value = lax.psum(value, axis)
            continue
        stride = 1
        while stride < size:
            pairs = [(index, index ^ stride) for index in range(size)]
            value = value + lax.ppermute(value, axis, pairs)
            stride *= 2
    return value


def inverse_factor(gram_block):
    factor = jnp.linalg.cholesky(gram_block)
    identity = jnp.eye(gram_block.shape[0], dtype=gram_block.dtype)
    return jax.scipy.linalg.solve_triangular(factor, identity, lower=True)


def shards(probe_block, prior_blocks, self_relatedness, tile_values, tile_index):
    col_count = lax.axis_size("col")
    block_count = prior_blocks.shape[0] + 1
    depth = probe_block.shape[0]
    highest = lax.Precision.HIGHEST
    basis = jnp.concatenate([prior_blocks, probe_block[None]], axis=0)
    flat_basis = basis.reshape(block_count * depth, basis.shape[2])
    wide_basis = flat_basis.astype(jnp.float32)
    gram_local = jnp.dot(flat_basis, flat_basis.T, preferred_element_type=jnp.float32)
    pairs = [(b, e) for b in range(block_count) for e in range(b + 1)]
    lower_local = jnp.stack(
        [gram_local[b * depth:(b + 1) * depth, e * depth:(e + 1) * depth] for b, e in pairs]
    )
    lower = hypercube_sum(lower_local, ("col", "row"))
    row_probes = lax.all_gather(probe_block, "col", axis=1, tiled=True)
    col_probes = lax.all_gather(probe_block, "row", axis=1, tiled=True)
    lower, row_probes, col_probes = lax.optimization_barrier((lower, row_probes, col_probes))
    gram = {pair: lower[n] for n, pair in enumerate(pairs)}
    inverses = [inverse_factor(gram[(b, b)]) for b in range(block_count)]
    row_part, col_part = tile_products(tile_values, tile_index, row_probes, col_probes, col_count)
    row_total = sum_rows(row_part)
    col_total = sum_columns(col_part)
    row_total, col_total, inverses = lax.optimization_barrier((row_total, col_total, inverses))
    product = self_relatedness[None, :] * probe_block.astype(jnp.float32) + row_total + col_total
    along_local = jnp.dot(wide_basis, product.T, precision=highest)
    along = hypercube_sum(along_local, ("col", "row"))
    solved = []
    for block_number in range(block_count):
        target = along[block_number * depth:(block_number + 1) * depth]
        for earlier in range(block_number):
            target = target - jnp.dot(gram[(block_number, earlier)], solved[earlier], precision=highest)
        inverse = inverses[block_number]
        half = jnp.dot(inverse, target, precision=highest)
        solved.append(jnp.dot(inverse.T, half, precision=highest))
    coefficients = jnp.concatenate(solved, axis=0)
    current = product - jnp.dot(coefficients.T, wide_basis, precision=highest)
    return (current, jnp.stack(solved))


def solution(mesh):
    in_specs = (
        P(None, ("row", "col")),
        P(None, None, ("row", "col")),
        P(("row", "col")),
        P(("row", "col"), None, None),
        P(("row", "col"), None),
    )
    out_specs = (P(None, ("row", "col")), P())
    return jax.shard_map(shards, mesh=mesh, in_specs=in_specs, out_specs=out_specs, check_vma=False)
```

```python
import jax
import jax.numpy as jnp
from jax import lax
from jax.sharding import PartitionSpec as P


def tile_products(tile_values, tile_index, row_probes, col_probes, col_count):
    tile_width = tile_values.shape[1]
    row_spans = row_probes.shape[1] // tile_width
    col_spans = col_probes.shape[1] // tile_width
    row_sum = None
    col_sum = None
    for slot_index in range(tile_values.shape[0]):
        current_tile = tile_values[slot_index]
        live = tile_index[slot_index, 2] > 0
        row_span = tile_index[slot_index, 0] % col_count
        col_span = tile_index[slot_index, 1] // col_count
        right = lax.dynamic_slice_in_dim(col_probes, col_span * tile_width, tile_width, 1)
        left = lax.dynamic_slice_in_dim(row_probes, row_span * tile_width, tile_width, 1)
        forward = lax.dot_general(
            right, current_tile, (((1,), (1,)), ((), ())), preferred_element_type=jnp.float32
        )
        mirror = jnp.dot(left, current_tile, preferred_element_type=jnp.float32)
        row_mask = (jnp.arange(row_spans) == row_span) & live
        col_mask = (jnp.arange(col_spans) == col_span) & live
        row_term = jnp.where(row_mask[None, :, None], forward[:, None, :], 0.0)
        col_term = jnp.where(col_mask[None, :, None], mirror[:, None, :], 0.0)
        row_sum = row_term if row_sum is None else row_sum + row_term
        col_sum = col_term if col_sum is None else col_sum + col_term
    depth = row_probes.shape[0]
    return row_sum.reshape(depth, row_probes.shape[1]), col_sum.reshape(depth, col_probes.shape[1])


def sum_rows(row_part):
    return lax.psum_scatter(row_part, "col", scatter_dimension=1, tiled=True)


def sum_columns(col_part):
    return lax.psum_scatter(col_part, "row", scatter_dimension=1, tiled=True)


def hypercube_sum(value, axes):
    for axis in axes:
        size = lax.axis_size(axis)
        if size & (size - 1):
            value = lax.psum(value, axis)
            continue
        stride = 1
        while stride < size:
            pairs = [(index, index ^ stride) for index in range(size)]
            value = value + lax.ppermute(value, axis, pairs)
            stride *= 2
    return value


def exchange_rounds(axes):
    rounds = []
    for axis in axes:
        size = lax.axis_size(axis)
        stride = 1
        while stride < size:
            rounds.append((axis, stride, size))
            stride *= 2
    return rounds


def halving_sum(value, axes):
    shape = value.shape
    flat = value.reshape(-1)
    done = []
    for axis, stride, size in exchange_rounds(axes):
        bit = lax.axis_index(axis) // stride % 2
        halves = flat.reshape(2, -1)
        keep = lax.dynamic_index_in_dim(halves, bit, 0, keepdims=False)
        give = lax.dynamic_index_in_dim(halves, 1 - bit, 0, keepdims=False)
        pairs = [(index, index ^ stride) for index in range(size)]
        flat = keep + lax.ppermute(give, axis, pairs)
        done.append((axis, stride, size, bit))
    for axis, stride, size, bit in reversed(done):
        pairs = [(index, index ^ stride) for index in range(size)]
        other = lax.ppermute(flat, axis, pairs)
        first = jnp.where(bit == 0, flat, other)
        second = jnp.where(bit == 0, other, flat)
        flat = jnp.concatenate([first, second])
    return flat.reshape(shape)


def inverse_factor(gram_block):
    factor = jnp.linalg.cholesky(gram_block)
    identity = jnp.eye(gram_block.shape[0], dtype=gram_block.dtype)
    return jax.scipy.linalg.solve_triangular(factor, identity, lower=True)


def shards(probe_block, prior_blocks, self_relatedness, tile_values, tile_index):
    col_count = lax.axis_size("col")
    block_count = prior_blocks.shape[0] + 1
    depth = probe_block.shape[0]
    highest = lax.Precision.HIGHEST
    basis = jnp.concatenate([prior_blocks, probe_block[None]], axis=0)
    flat_basis = basis.reshape(block_count * depth, basis.shape[2])
    wide_basis = flat_basis.astype(jnp.float32)
    gram_local = jnp.dot(flat_basis, flat_basis.T, preferred_element_type=jnp.float32)
    pairs = [(b, e) for b in range(block_count) for e in range(b + 1)]
    lower_local = jnp.stack(
        [gram_local[b * depth:(b + 1) * depth, e * depth:(e + 1) * depth] for b, e in pairs]
    )
    lower = halving_sum(lower_local, ("col", "row"))
    row_probes = lax.all_gather(probe_block, "col", axis=1, tiled=True)
    col_probes = lax.all_gather(probe_block, "row", axis=1, tiled=True)
    lower, row_probes, col_probes = lax.optimization_barrier((lower, row_probes, col_probes))
    gram = {pair: lower[n] for n, pair in enumerate(pairs)}
    inverses = [inverse_factor(gram[(b, b)]) for b in range(block_count)]
    row_part, col_part = tile_products(tile_values, tile_index, row_probes, col_probes, col_count)
    row_total = sum_rows(row_part)
    col_total = sum_columns(col_part)
    row_total, col_total, inverses = lax.optimization_barrier((row_total, col_total, inverses))
    product = self_relatedness[None, :] * probe_block.astype(jnp.float32) + row_total + col_total
    along_local = jnp.dot(wide_basis, product.T, precision=highest)
    along = hypercube_sum(along_local, ("col", "row"))
    solved = []
    for block_number in range(block_count):
        target = along[block_number * depth:(block_number + 1) * depth]
        for earlier in range(block_number):
            target = target - jnp.dot(gram[(block_number, earlier)], solved[earlier], precision=highest)
        inverse = inverses[block_number]
        half = jnp.dot(inverse, target, precision=highest)
        solved.append(jnp.dot(inverse.T, half, precision=highest))
    coefficients = jnp.concatenate(solved, axis=0)
    current = product - jnp.dot(coefficients.T, wide_basis, precision=highest)
    return (current, jnp.stack(solved))


def solution(mesh):
    in_specs = (
        P(None, ("row", "col")),
        P(None, None, ("row", "col")),
        P(("row", "col")),
        P(("row", "col"), None, None),
        P(("row", "col"), None),
    )
    out_specs = (P(None, ("row", "col")), P())
    return jax.shard_map(shards, mesh=mesh, in_specs=in_specs, out_specs=out_specs, check_vma=False)
```

```python
import jax
import jax.numpy as jnp
from jax import lax
from jax.sharding import PartitionSpec as P


def tile_products(tile_values, tile_index, row_probes, col_probes, col_count):
    tile_width = tile_values.shape[1]
    row_spans = row_probes.shape[1] // tile_width
    col_spans = col_probes.shape[1] // tile_width
    forwards, mirrors, row_spans_of, col_spans_of = [], [], [], []
    for slot_index in range(tile_values.shape[0]):
        current_tile = tile_values[slot_index]
        live = tile_index[slot_index, 2] > 0
        row_span = tile_index[slot_index, 0] % col_count
        col_span = tile_index[slot_index, 1] // col_count
        right = lax.dynamic_slice_in_dim(col_probes, col_span * tile_width, tile_width, 1)
        left = lax.dynamic_slice_in_dim(row_probes, row_span * tile_width, tile_width, 1)
        forward = lax.dot_general(
            right, current_tile, (((1,), (1,)), ((), ())), preferred_element_type=jnp.float32
        )
        mirror = jnp.dot(left, current_tile, preferred_element_type=jnp.float32)
        forwards.append(forward)
        mirrors.append(mirror)
        row_spans_of.append(jnp.where(live, row_span, -1))
        col_spans_of.append(jnp.where(live, col_span, -1))
    row_part = spread_spans(forwards, row_spans_of, row_spans)
    col_part = spread_spans(mirrors, col_spans_of, col_spans)
    return row_part, col_part


def spread_spans(terms, spans_of, span_count):
    pieces = []
    for span in range(span_count):
        piece = None
        for term, span_of in zip(terms, spans_of):
            part = jnp.where(span_of == span, term, 0.0)
            piece = part if piece is None else piece + part
        pieces.append(piece)
    return jnp.concatenate(pieces, axis=1)


def sum_rows(row_part):
    return lax.psum_scatter(row_part, "col", scatter_dimension=1, tiled=True)


def sum_columns(col_part):
    return lax.psum_scatter(col_part, "row", scatter_dimension=1, tiled=True)


def hypercube_sum(value, axes):
    for axis in axes:
        size = lax.axis_size(axis)
        if size & (size - 1):
            value = lax.psum(value, axis)
            continue
        stride = 1
        while stride < size:
            pairs = [(index, index ^ stride) for index in range(size)]
            value = value + lax.ppermute(value, axis, pairs)
            stride *= 2
    return value


def radix_sum(value, axes, radix=4):
    for axis in axes:
        size = lax.axis_size(axis)
        stride = 1
        while stride < size:
            width = radix if size % (stride * radix) == 0 else 2
            position = lax.axis_index(axis) // stride % width
            received = [value]
            for distance in range(1, width):
                pairs = []
                for index in range(size):
                    member = index // stride % width
                    partner = index + ((member ^ distance) - member) * stride
                    pairs.append((index, partner))
                received.append(lax.ppermute(value, axis, pairs))
            stacked = jnp.stack(received)
            ordered = [
                lax.dynamic_index_in_dim(stacked, position ^ member, 0, keepdims=False)
                for member in range(width)
            ]
            while len(ordered) > 1:
                ordered = [ordered[n] + ordered[n + 1] for n in range(0, len(ordered), 2)]
            value = ordered[0]
            stride *= width
    return value


def exchange_rounds(axes):
    rounds = []
    for axis in axes:
        size = lax.axis_size(axis)
        stride = 1
        while stride < size:
            rounds.append((axis, stride, size))
            stride *= 2
    return rounds


def halving_sum(value, axes):
    shape = value.shape
    flat = value.reshape(-1)
    done = []
    for axis, stride, size in exchange_rounds(axes):
        bit = lax.axis_index(axis) // stride % 2
        halves = flat.reshape(2, -1)
        keep = lax.dynamic_index_in_dim(halves, bit, 0, keepdims=False)
        give = lax.dynamic_index_in_dim(halves, 1 - bit, 0, keepdims=False)
        pairs = [(index, index ^ stride) for index in range(size)]
        flat = keep + lax.ppermute(give, axis, pairs)
        done.append((axis, stride, size, bit))
    for axis, stride, size, bit in reversed(done):
        pairs = [(index, index ^ stride) for index in range(size)]
        other = lax.ppermute(flat, axis, pairs)
        first = jnp.where(bit == 0, flat, other)
        second = jnp.where(bit == 0, other, flat)
        flat = jnp.concatenate([first, second])
    return flat.reshape(shape)


def inverse_factor(gram_block):
    factor = jnp.linalg.cholesky(gram_block)
    identity = jnp.eye(gram_block.shape[0], dtype=gram_block.dtype)
    return jax.scipy.linalg.solve_triangular(factor, identity, lower=True)


def shards(probe_block, prior_blocks, self_relatedness, tile_values, tile_index):
    col_count = lax.axis_size("col")
    block_count = prior_blocks.shape[0] + 1
    depth = probe_block.shape[0]
    highest = lax.Precision.HIGHEST
    basis = jnp.concatenate([prior_blocks, probe_block[None]], axis=0)
    flat_basis = basis.reshape(block_count * depth, basis.shape[2])
    wide_basis = flat_basis.astype(jnp.float32)
    gram_local = jnp.dot(flat_basis, flat_basis.T, preferred_element_type=jnp.float32)
    pairs = [(b, e) for b in range(block_count) for e in range(b + 1)]
    lower_local = jnp.stack(
        [gram_local[b * depth:(b + 1) * depth, e * depth:(e + 1) * depth] for b, e in pairs]
    )
    lower = halving_sum(lower_local, ("col", "row"))
    row_probes = lax.all_gather(probe_block, "col", axis=1, tiled=True)
    col_probes = lax.all_gather(probe_block, "row", axis=1, tiled=True)
    lower, row_probes, col_probes = lax.optimization_barrier((lower, row_probes, col_probes))
    gram = {pair: lower[n] for n, pair in enumerate(pairs)}
    inverses = [inverse_factor(gram[(b, b)]) for b in range(block_count)]
    row_part, col_part = tile_products(tile_values, tile_index, row_probes, col_probes, col_count)
    row_total = sum_rows(row_part)
    col_total = sum_columns(col_part)
    row_total, col_total, inverses = lax.optimization_barrier((row_total, col_total, inverses))
    product = self_relatedness[None, :] * probe_block.astype(jnp.float32) + row_total + col_total
    along_local = jnp.dot(wide_basis, product.T, precision=highest)
    along = radix_sum(along_local, ("col", "row"))
    solved = []
    for block_number in range(block_count):
        target = along[block_number * depth:(block_number + 1) * depth]
        for earlier in range(block_number):
            target = target - jnp.dot(gram[(block_number, earlier)], solved[earlier], precision=highest)
        inverse = inverses[block_number]
        half = jnp.dot(inverse, target, precision=highest)
        solved.append(jnp.dot(inverse.T, half, precision=highest))
    coefficients = jnp.concatenate(solved, axis=0)
    current = product - jnp.dot(coefficients.T, wide_basis, precision=highest)
    return (current, jnp.stack(solved))


def solution(mesh):
    in_specs = (
        P(None, ("row", "col")),
        P(None, None, ("row", "col")),
        P(("row", "col")),
        P(("row", "col"), None, None),
        P(("row", "col"), None),
    )
    out_specs = (P(None, ("row", "col")), P())
    return jax.shard_map(shards, mesh=mesh, in_specs=in_specs, out_specs=out_specs, check_vma=False)
```

```python
import jax
import jax.numpy as jnp
from jax import lax
from jax.sharding import PartitionSpec as P


def tile_products(tile_values, tile_index, row_probes, col_probes, col_count):
    tile_width = tile_values.shape[1]
    row_spans = row_probes.shape[1] // tile_width
    col_spans = col_probes.shape[1] // tile_width
    forwards, mirrors, row_spans_of, col_spans_of = [], [], [], []
    for slot_index in range(tile_values.shape[0]):
        current_tile = tile_values[slot_index]
        live = tile_index[slot_index, 2] > 0
        row_span = tile_index[slot_index, 0] % col_count
        col_span = tile_index[slot_index, 1] // col_count
        right = lax.dynamic_slice_in_dim(col_probes, col_span * tile_width, tile_width, 1)
        left = lax.dynamic_slice_in_dim(row_probes, row_span * tile_width, tile_width, 1)
        forward = lax.dot_general(
            right, current_tile, (((1,), (1,)), ((), ())), preferred_element_type=jnp.float32
        )
        mirror = jnp.dot(left, current_tile, preferred_element_type=jnp.float32)
        forwards.append(forward)
        mirrors.append(mirror)
        row_spans_of.append(jnp.where(live, row_span, -1))
        col_spans_of.append(jnp.where(live, col_span, -1))
    row_part = jnp.stack(spread_spans(forwards, row_spans_of, row_spans))
    col_part = jnp.concatenate(spread_spans(mirrors, col_spans_of, col_spans), axis=1)
    return row_part, col_part


def spread_spans(terms, spans_of, span_count):
    pieces = []
    for span in range(span_count):
        piece = None
        for term, span_of in zip(terms, spans_of):
            part = jnp.where(span_of == span, term, 0.0)
            piece = part if piece is None else piece + part
        pieces.append(piece)
    return pieces


def sum_rows(row_part):
    size = lax.axis_size("col")
    if size & (size - 1):
        flat = jnp.concatenate(list(row_part), axis=1)
        return lax.psum_scatter(flat, "col", scatter_dimension=1, tiled=True)
    stride = 1
    while stride < size:
        bit = lax.axis_index("col") // stride % 2
        grouped = row_part.reshape(row_part.shape[0] // 2, 2, *row_part.shape[1:])
        keep = lax.dynamic_index_in_dim(grouped, bit, 1, keepdims=False)
        give = lax.dynamic_index_in_dim(grouped, 1 - bit, 1, keepdims=False)
        pairs = [(index, index ^ stride) for index in range(size)]
        row_part = keep + lax.ppermute(give, "col", pairs)
        stride *= 2
    return row_part[0]


def sum_columns(col_part):
    return lax.psum_scatter(col_part, "row", scatter_dimension=1, tiled=True)


def hypercube_sum(value, axes):
    for axis in axes:
        size = lax.axis_size(axis)
        if size & (size - 1):
            value = lax.psum(value, axis)
            continue
        stride = 1
        while stride < size:
            pairs = [(index, index ^ stride) for index in range(size)]
            value = value + lax.ppermute(value, axis, pairs)
            stride *= 2
    return value


def radix_sum(value, axes, radix=4):
    for axis in axes:
        size = lax.axis_size(axis)
        stride = 1
        while stride < size:
            width = radix if size % (stride * radix) == 0 else 2
            position = lax.axis_index(axis) // stride % width
            received = [value]
            for distance in range(1, width):
                pairs = []
                for index in range(size):
                    member = index // stride % width
                    partner = index + ((member ^ distance) - member) * stride
                    pairs.append((index, partner))
                received.append(lax.ppermute(value, axis, pairs))
            stacked = jnp.stack(received)
            ordered = [
                lax.dynamic_index_in_dim(stacked, position ^ member, 0, keepdims=False)
                for member in range(width)
            ]
            while len(ordered) > 1:
                ordered = [ordered[n] + ordered[n + 1] for n in range(0, len(ordered), 2)]
            value = ordered[0]
            stride *= width
    return value


def exchange_rounds(axes):
    rounds = []
    for axis in axes:
        size = lax.axis_size(axis)
        stride = 1
        while stride < size:
            rounds.append((axis, stride, size))
            stride *= 2
    return rounds


def halving_sum(value, axes):
    shape = value.shape
    flat = value.reshape(-1)
    done = []
    for axis, stride, size in exchange_rounds(axes):
        bit = lax.axis_index(axis) // stride % 2
        halves = flat.reshape(2, -1)
        keep = lax.dynamic_index_in_dim(halves, bit, 0, keepdims=False)
        give = lax.dynamic_index_in_dim(halves, 1 - bit, 0, keepdims=False)
        pairs = [(index, index ^ stride) for index in range(size)]
        flat = keep + lax.ppermute(give, axis, pairs)
        done.append((axis, stride, size, bit))
    for axis, stride, size, bit in reversed(done):
        pairs = [(index, index ^ stride) for index in range(size)]
        other = lax.ppermute(flat, axis, pairs)
        first = jnp.where(bit == 0, flat, other)
        second = jnp.where(bit == 0, other, flat)
        flat = jnp.concatenate([first, second])
    return flat.reshape(shape)


def inverse_factor(gram_block):
    factor = jnp.linalg.cholesky(gram_block)
    identity = jnp.eye(gram_block.shape[0], dtype=gram_block.dtype)
    return jax.scipy.linalg.solve_triangular(factor, identity, lower=True)


def shards(probe_block, prior_blocks, self_relatedness, tile_values, tile_index):
    col_count = lax.axis_size("col")
    block_count = prior_blocks.shape[0] + 1
    depth = probe_block.shape[0]
    highest = lax.Precision.HIGHEST
    basis = jnp.concatenate([prior_blocks, probe_block[None]], axis=0)
    flat_basis = basis.reshape(block_count * depth, basis.shape[2])
    wide_basis = flat_basis.astype(jnp.float32)
    gram_local = jnp.dot(flat_basis, flat_basis.T, preferred_element_type=jnp.float32)
    pairs = [(b, e) for b in range(block_count) for e in range(b + 1)]
    lower_local = jnp.stack(
        [gram_local[b * depth:(b + 1) * depth, e * depth:(e + 1) * depth] for b, e in pairs]
    )
    lower = halving_sum(lower_local, ("col", "row"))
    row_probes = lax.all_gather(probe_block, "col", axis=1, tiled=True)
    col_probes = lax.all_gather(probe_block, "row", axis=1, tiled=True)
    lower, row_probes, col_probes = lax.optimization_barrier((lower, row_probes, col_probes))
    gram = {pair: lower[n] for n, pair in enumerate(pairs)}
    inverses = [inverse_factor(gram[(b, b)]) for b in range(block_count)]
    row_part, col_part = tile_products(tile_values, tile_index, row_probes, col_probes, col_count)
    row_total = sum_rows(row_part)
    col_total = sum_columns(col_part)
    row_total, col_total, inverses = lax.optimization_barrier((row_total, col_total, inverses))
    product = self_relatedness[None, :] * probe_block.astype(jnp.float32) + row_total + col_total
    along_local = jnp.dot(wide_basis, product.T, precision=highest)
    along = radix_sum(along_local, ("col", "row"))
    solved = []
    for block_number in range(block_count):
        target = along[block_number * depth:(block_number + 1) * depth]
        for earlier in range(block_number):
            target = target - jnp.dot(gram[(block_number, earlier)], solved[earlier], precision=highest)
        inverse = inverses[block_number]
        half = jnp.dot(inverse, target, precision=highest)
        solved.append(jnp.dot(inverse.T, half, precision=highest))
    coefficients = jnp.concatenate(solved, axis=0)
    current = product - jnp.dot(coefficients.T, wide_basis, precision=highest)
    return (current, jnp.stack(solved))


def solution(mesh):
    in_specs = (
        P(None, ("row", "col")),
        P(None, None, ("row", "col")),
        P(("row", "col")),
        P(("row", "col"), None, None),
        P(("row", "col"), None),
    )
    out_specs = (P(None, ("row", "col")), P())
    return jax.shard_map(shards, mesh=mesh, in_specs=in_specs, out_specs=out_specs, check_vma=False)
```

```python
import jax
import jax.numpy as jnp
from jax import lax
from jax.sharding import PartitionSpec as P


def tile_products(tile_values, tile_index, row_probes, col_probes, col_count):
    tile_width = tile_values.shape[1]
    row_spans = row_probes.shape[1] // tile_width
    col_spans = col_probes.shape[1] // tile_width
    forwards, mirrors, row_spans_of, col_spans_of = [], [], [], []
    for slot_index in range(tile_values.shape[0]):
        current_tile = tile_values[slot_index]
        live = tile_index[slot_index, 2] > 0
        row_span = tile_index[slot_index, 0] % col_count
        col_span = tile_index[slot_index, 1] // col_count
        right = lax.dynamic_slice_in_dim(col_probes, col_span * tile_width, tile_width, 1)
        left = lax.dynamic_slice_in_dim(row_probes, row_span * tile_width, tile_width, 1)
        forward = lax.dot_general(
            right, current_tile, (((1,), (1,)), ((), ())), preferred_element_type=jnp.float32
        )
        mirror = jnp.dot(left, current_tile, preferred_element_type=jnp.float32)
        forwards.append(forward)
        mirrors.append(mirror)
        row_spans_of.append(jnp.where(live, row_span, -1))
        col_spans_of.append(jnp.where(live, col_span, -1))
    row_part = jnp.stack(spread_spans(forwards, row_spans_of, row_spans))
    col_part = jnp.concatenate(spread_spans(mirrors, col_spans_of, col_spans), axis=1)
    return row_part, col_part


def spread_spans(terms, spans_of, span_count):
    pieces = []
    for span in range(span_count):
        piece = None
        for term, span_of in zip(terms, spans_of):
            part = jnp.where(span_of == span, term, 0.0)
            piece = part if piece is None else piece + part
        pieces.append(piece)
    return pieces


def sum_rows(row_part):
    size = lax.axis_size("col")
    if size & (size - 1):
        flat = jnp.concatenate(list(row_part), axis=1)
        return lax.psum_scatter(flat, "col", scatter_dimension=1, tiled=True)
    stride = 1
    while stride < size:
        bit = lax.axis_index("col") // stride % 2
        grouped = row_part.reshape(row_part.shape[0] // 2, 2, *row_part.shape[1:])
        keep = lax.dynamic_index_in_dim(grouped, bit, 1, keepdims=False)
        give = lax.dynamic_index_in_dim(grouped, 1 - bit, 1, keepdims=False)
        pairs = [(index, index ^ stride) for index in range(size)]
        row_part = keep + lax.ppermute(give, "col", pairs)
        stride *= 2
    return row_part[0]


def sum_columns(col_part):
    return lax.psum_scatter(col_part, "row", scatter_dimension=1, tiled=True)


def hypercube_sum(value, axes):
    for axis in axes:
        size = lax.axis_size(axis)
        if size & (size - 1):
            value = lax.psum(value, axis)
            continue
        stride = 1
        while stride < size:
            pairs = [(index, index ^ stride) for index in range(size)]
            value = value + lax.ppermute(value, axis, pairs)
            stride *= 2
    return value


def radix_sum(value, axes, radix=4):
    for axis in axes:
        size = lax.axis_size(axis)
        stride = 1
        while stride < size:
            width = radix if size % (stride * radix) == 0 else 2
            position = lax.axis_index(axis) // stride % width
            received = [value]
            for distance in range(1, width):
                pairs = []
                for index in range(size):
                    member = index // stride % width
                    partner = index + ((member ^ distance) - member) * stride
                    pairs.append((index, partner))
                received.append(lax.ppermute(value, axis, pairs))
            stacked = jnp.stack(received)
            ordered = [
                lax.dynamic_index_in_dim(stacked, position ^ member, 0, keepdims=False)
                for member in range(width)
            ]
            while len(ordered) > 1:
                ordered = [ordered[n] + ordered[n + 1] for n in range(0, len(ordered), 2)]
            value = ordered[0]
            stride *= width
    return value


def exchange_rounds(axes):
    rounds = []
    for axis in axes:
        size = lax.axis_size(axis)
        stride = 1
        while stride < size:
            rounds.append((axis, stride, size))
            stride *= 2
    return rounds


def halving_sum(value, axes):
    shape = value.shape
    flat = value.reshape(-1)
    done = []
    for axis, stride, size in exchange_rounds(axes):
        bit = lax.axis_index(axis) // stride % 2
        halves = flat.reshape(2, -1)
        keep = lax.dynamic_index_in_dim(halves, bit, 0, keepdims=False)
        give = lax.dynamic_index_in_dim(halves, 1 - bit, 0, keepdims=False)
        pairs = [(index, index ^ stride) for index in range(size)]
        flat = keep + lax.ppermute(give, axis, pairs)
        done.append((axis, stride, size, bit))
    for axis, stride, size, bit in reversed(done):
        pairs = [(index, index ^ stride) for index in range(size)]
        other = lax.ppermute(flat, axis, pairs)
        first = jnp.where(bit == 0, flat, other)
        second = jnp.where(bit == 0, other, flat)
        flat = jnp.concatenate([first, second])
    return flat.reshape(shape)


def inverse_factors(gram_blocks):
    factors = jnp.linalg.cholesky(gram_blocks)
    identity = jnp.broadcast_to(jnp.eye(gram_blocks.shape[1], dtype=gram_blocks.dtype), gram_blocks.shape)
    return jax.scipy.linalg.solve_triangular(factors, identity, lower=True)


def shards(probe_block, prior_blocks, self_relatedness, tile_values, tile_index):
    col_count = lax.axis_size("col")
    block_count = prior_blocks.shape[0] + 1
    depth = probe_block.shape[0]
    highest = lax.Precision.HIGHEST
    basis = jnp.concatenate([prior_blocks, probe_block[None]], axis=0)
    flat_basis = basis.reshape(block_count * depth, basis.shape[2])
    wide_basis = flat_basis.astype(jnp.float32)
    gram_local = jnp.dot(flat_basis, flat_basis.T, preferred_element_type=jnp.float32)
    pairs = [(b, e) for b in range(block_count) for e in range(b + 1)]
    lower_local = jnp.stack(
        [gram_local[b * depth:(b + 1) * depth, e * depth:(e + 1) * depth] for b, e in pairs]
    )
    lower = halving_sum(lower_local, ("col", "row"))
    row_probes = lax.all_gather(probe_block, "col", axis=1, tiled=True)
    col_probes = lax.all_gather(probe_block, "row", axis=1, tiled=True)
    lower, row_probes, col_probes = lax.optimization_barrier((lower, row_probes, col_probes))
    gram = {pair: lower[n] for n, pair in enumerate(pairs)}
    inverses = inverse_factors(jnp.stack([gram[(b, b)] for b in range(block_count)]))
    row_part, col_part = tile_products(tile_values, tile_index, row_probes, col_probes, col_count)
    row_total = sum_rows(row_part)
    col_total = sum_columns(col_part)
    row_total, col_total, inverses = lax.optimization_barrier((row_total, col_total, inverses))
    product = self_relatedness[None, :] * probe_block.astype(jnp.float32) + row_total + col_total
    along_local = jnp.dot(wide_basis, product.T, precision=highest)
    along = radix_sum(along_local, ("col", "row"))
    solved = []
    for block_number in range(block_count):
        target = along[block_number * depth:(block_number + 1) * depth]
        for earlier in range(block_number):
            target = target - jnp.dot(gram[(block_number, earlier)], solved[earlier], precision=highest)
        inverse = inverses[block_number]
        half = jnp.dot(inverse, target, precision=highest)
        solved.append(jnp.dot(inverse.T, half, precision=highest))
    coefficients = jnp.concatenate(solved, axis=0)
    current = product - jnp.dot(coefficients.T, wide_basis, precision=highest)
    return (current, jnp.stack(solved))


def solution(mesh):
    in_specs = (
        P(None, ("row", "col")),
        P(None, None, ("row", "col")),
        P(("row", "col")),
        P(("row", "col"), None, None),
        P(("row", "col"), None),
    )
    out_specs = (P(None, ("row", "col")), P())
    return jax.shard_map(shards, mesh=mesh, in_specs=in_specs, out_specs=out_specs, check_vma=False)
```

```python
import jax
import jax.numpy as jnp
from jax import lax
from jax.sharding import PartitionSpec as P


def tile_products(tile_values, tile_index, row_probes, col_probes, col_count):
    tile_width = tile_values.shape[1]
    row_spans = row_probes.shape[1] // tile_width
    col_spans = col_probes.shape[1] // tile_width
    forwards, mirrors, row_spans_of, col_spans_of = [], [], [], []
    for slot_index in range(tile_values.shape[0]):
        current_tile = tile_values[slot_index]
        live = tile_index[slot_index, 2] > 0
        row_span = tile_index[slot_index, 0] % col_count
        col_span = tile_index[slot_index, 1] // col_count
        right = lax.dynamic_slice_in_dim(col_probes, col_span * tile_width, tile_width, 1)
        left = lax.dynamic_slice_in_dim(row_probes, row_span * tile_width, tile_width, 1)
        forward = lax.dot_general(
            right, current_tile, (((1,), (1,)), ((), ())), preferred_element_type=jnp.float32
        )
        mirror = jnp.dot(left, current_tile, preferred_element_type=jnp.float32)
        forwards.append(forward)
        mirrors.append(mirror)
        row_spans_of.append(jnp.where(live, row_span, -1))
        col_spans_of.append(jnp.where(live, col_span, -1))
    row_part = jnp.stack(spread_spans(forwards, row_spans_of, row_spans))
    col_part = jnp.concatenate(spread_spans(mirrors, col_spans_of, col_spans), axis=1)
    return row_part, col_part


def spread_spans(terms, spans_of, span_count):
    pieces = []
    for span in range(span_count):
        piece = None
        for term, span_of in zip(terms, spans_of):
            part = jnp.where(span_of == span, term, 0.0)
            piece = part if piece is None else piece + part
        pieces.append(piece)
    return pieces


def sum_rows(row_part):
    size = lax.axis_size("col")
    if size & (size - 1):
        flat = jnp.concatenate(list(row_part), axis=1)
        return lax.psum_scatter(flat, "col", scatter_dimension=1, tiled=True)
    stride = 1
    while stride < size:
        bit = lax.axis_index("col") // stride % 2
        grouped = row_part.reshape(row_part.shape[0] // 2, 2, *row_part.shape[1:])
        keep = lax.dynamic_index_in_dim(grouped, bit, 1, keepdims=False)
        give = lax.dynamic_index_in_dim(grouped, 1 - bit, 1, keepdims=False)
        pairs = [(index, index ^ stride) for index in range(size)]
        row_part = keep + lax.ppermute(give, "col", pairs)
        stride *= 2
    return row_part[0]


def sum_columns(col_part):
    return lax.psum_scatter(col_part, "row", scatter_dimension=1, tiled=True)


def hypercube_sum(value, axes):
    for axis in axes:
        size = lax.axis_size(axis)
        if size & (size - 1):
            value = lax.psum(value, axis)
            continue
        stride = 1
        while stride < size:
            pairs = [(index, index ^ stride) for index in range(size)]
            value = value + lax.ppermute(value, axis, pairs)
            stride *= 2
    return value


def radix_sum(value, axes, radix=4):
    for axis in axes:
        size = lax.axis_size(axis)
        stride = 1
        while stride < size:
            width = radix if size % (stride * radix) == 0 else 2
            position = lax.axis_index(axis) // stride % width
            received = [value]
            for distance in range(1, width):
                pairs = []
                for index in range(size):
                    member = index // stride % width
                    partner = index + ((member ^ distance) - member) * stride
                    pairs.append((index, partner))
                received.append(lax.ppermute(value, axis, pairs))
            stacked = jnp.stack(received)
            ordered = [
                lax.dynamic_index_in_dim(stacked, position ^ member, 0, keepdims=False)
                for member in range(width)
            ]
            while len(ordered) > 1:
                ordered = [ordered[n] + ordered[n + 1] for n in range(0, len(ordered), 2)]
            value = ordered[0]
            stride *= width
    return value


def quarter_sum(value, axes, radix=4):
    shape = value.shape
    flat = value.reshape(-1)
    done = []
    for axis in axes:
        size = lax.axis_size(axis)
        stride = 1
        while stride < size:
            width = radix if size % (stride * radix) == 0 else 2
            position = lax.axis_index(axis) // stride % width
            parts = flat.reshape(width, -1)
            terms = [lax.dynamic_index_in_dim(parts, position, 0, keepdims=False)]
            for distance in range(1, width):
                give = lax.dynamic_index_in_dim(parts, position ^ distance, 0, keepdims=False)
                terms.append(lax.ppermute(give, axis, group_pairs(size, stride, width, distance)))
            flat = sum(terms[1:], terms[0])
            done.append((axis, size, stride, width, position))
            stride *= width
    for axis, size, stride, width, position in reversed(done):
        terms = [flat]
        for distance in range(1, width):
            terms.append(lax.ppermute(flat, axis, group_pairs(size, stride, width, distance)))
        stacked = jnp.stack(terms)
        flat = jnp.concatenate(
            [lax.dynamic_index_in_dim(stacked, position ^ member, 0, keepdims=False) for member in range(width)]
        )
    return flat.reshape(shape)


def group_pairs(size, stride, width, distance):
    pairs = []
    for index in range(size):
        member = index // stride % width
        pairs.append((index, index + ((member ^ distance) - member) * stride))
    return pairs


def exchange_rounds(axes):
    rounds = []
    for axis in axes:
        size = lax.axis_size(axis)
        stride = 1
        while stride < size:
            rounds.append((axis, stride, size))
            stride *= 2
    return rounds


def halving_sum(value, axes):
    shape = value.shape
    flat = value.reshape(-1)
    done = []
    for axis, stride, size in exchange_rounds(axes):
        bit = lax.axis_index(axis) // stride % 2
        halves = flat.reshape(2, -1)
        keep = lax.dynamic_index_in_dim(halves, bit, 0, keepdims=False)
        give = lax.dynamic_index_in_dim(halves, 1 - bit, 0, keepdims=False)
        pairs = [(index, index ^ stride) for index in range(size)]
        flat = keep + lax.ppermute(give, axis, pairs)
        done.append((axis, stride, size, bit))
    for axis, stride, size, bit in reversed(done):
        pairs = [(index, index ^ stride) for index in range(size)]
        other = lax.ppermute(flat, axis, pairs)
        first = jnp.where(bit == 0, flat, other)
        second = jnp.where(bit == 0, other, flat)
        flat = jnp.concatenate([first, second])
    return flat.reshape(shape)


def inverse_factors(gram_blocks):
    factors = jnp.linalg.cholesky(gram_blocks)
    identity = jnp.broadcast_to(jnp.eye(gram_blocks.shape[1], dtype=gram_blocks.dtype), gram_blocks.shape)
    return jax.scipy.linalg.solve_triangular(factors, identity, lower=True)


def shards(probe_block, prior_blocks, self_relatedness, tile_values, tile_index):
    col_count = lax.axis_size("col")
    block_count = prior_blocks.shape[0] + 1
    depth = probe_block.shape[0]
    highest = lax.Precision.HIGHEST
    basis = jnp.concatenate([prior_blocks, probe_block[None]], axis=0)
    flat_basis = basis.reshape(block_count * depth, basis.shape[2])
    wide_basis = flat_basis.astype(jnp.float32)
    gram_local = jnp.dot(flat_basis, flat_basis.T, preferred_element_type=jnp.float32)
    pairs = [(b, e) for b in range(block_count) for e in range(b + 1)]
    lower_local = jnp.stack(
        [gram_local[b * depth:(b + 1) * depth, e * depth:(e + 1) * depth] for b, e in pairs]
    )
    lower = quarter_sum(lower_local, ("col", "row"))
    row_probes = lax.all_gather(probe_block, "col", axis=1, tiled=True)
    col_probes = lax.all_gather(probe_block, "row", axis=1, tiled=True)
    gram = {pair: lower[n] for n, pair in enumerate(pairs)}
    inverses = inverse_factors(jnp.stack([gram[(b, b)] for b in range(block_count)]))
    inverses, row_probes, col_probes = lax.optimization_barrier((inverses, row_probes, col_probes))
    row_part, col_part = tile_products(tile_values, tile_index, row_probes, col_probes, col_count)
    row_total = sum_rows(row_part)
    col_total = sum_columns(col_part)
    product = self_relatedness[None, :] * probe_block.astype(jnp.float32) + row_total + col_total
    along_local = jnp.dot(wide_basis, product.T, precision=highest)
    along = radix_sum(along_local, ("col", "row"))
    solved = []
    for block_number in range(block_count):
        target = along[block_number * depth:(block_number + 1) * depth]
        for earlier in range(block_number):
            target = target - jnp.dot(gram[(block_number, earlier)], solved[earlier], precision=highest)
        inverse = inverses[block_number]
        half = jnp.dot(inverse, target, precision=highest)
        solved.append(jnp.dot(inverse.T, half, precision=highest))
    coefficients = jnp.concatenate(solved, axis=0)
    current = product - jnp.dot(coefficients.T, wide_basis, precision=highest)
    return (current, jnp.stack(solved))


def solution(mesh):
    in_specs = (
        P(None, ("row", "col")),
        P(None, None, ("row", "col")),
        P(("row", "col")),
        P(("row", "col"), None, None),
        P(("row", "col"), None),
    )
    out_specs = (P(None, ("row", "col")), P())
    return jax.shard_map(shards, mesh=mesh, in_specs=in_specs, out_specs=out_specs, check_vma=False)
```

```python
import jax
import jax.numpy as jnp
from jax import lax
from jax.sharding import PartitionSpec as P


def tile_products(tile_values, tile_index, row_probes, col_probes, col_count):
    tile_width = tile_values.shape[1]
    row_spans = row_probes.shape[1] // tile_width
    col_spans = col_probes.shape[0]
    forwards, mirrors, row_spans_of, col_spans_of = [], [], [], []
    for slot_index in range(tile_values.shape[0]):
        current_tile = tile_values[slot_index]
        live = tile_index[slot_index, 2] > 0
        row_span = tile_index[slot_index, 0] % col_count
        col_span = tile_index[slot_index, 1] // col_count
        right = lax.dynamic_index_in_dim(col_probes, col_span, 0, keepdims=False)
        left = lax.dynamic_slice_in_dim(row_probes, row_span * tile_width, tile_width, 1)
        forward = lax.dot_general(
            right, current_tile, (((1,), (1,)), ((), ())), preferred_element_type=jnp.float32
        )
        mirror = jnp.dot(left, current_tile, preferred_element_type=jnp.float32)
        forwards.append(forward)
        mirrors.append(mirror)
        row_spans_of.append(jnp.where(live, row_span, -1))
        col_spans_of.append(jnp.where(live, col_span, -1))
    row_part = jnp.stack(spread_spans(forwards, row_spans_of, row_spans))
    col_part = jnp.concatenate(spread_spans(mirrors, col_spans_of, col_spans), axis=1)
    return row_part, col_part


def spread_spans(terms, spans_of, span_count):
    pieces = []
    for span in range(span_count):
        piece = None
        for term, span_of in zip(terms, spans_of):
            part = jnp.where(span_of == span, term, 0.0)
            piece = part if piece is None else piece + part
        pieces.append(piece)
    return pieces


def sum_rows(row_part):
    size = lax.axis_size("col")
    if size & (size - 1):
        flat = jnp.concatenate(list(row_part), axis=1)
        return lax.psum_scatter(flat, "col", scatter_dimension=1, tiled=True)
    stride = 1
    while stride < size:
        bit = lax.axis_index("col") // stride % 2
        grouped = row_part.reshape(row_part.shape[0] // 2, 2, *row_part.shape[1:])
        keep = lax.dynamic_index_in_dim(grouped, bit, 1, keepdims=False)
        give = lax.dynamic_index_in_dim(grouped, 1 - bit, 1, keepdims=False)
        pairs = [(index, index ^ stride) for index in range(size)]
        row_part = keep + lax.ppermute(give, "col", pairs)
        stride *= 2
    return row_part[0]


def gather_spans(block, axis):
    size = lax.axis_size(axis)
    if size & (size - 1):
        return lax.all_gather(block, axis, axis=0, tiled=False)
    spans = block[None]
    stride = 1
    while stride < size:
        bit = lax.axis_index(axis) // stride % 2
        pairs = [(index, index ^ stride) for index in range(size)]
        other = lax.ppermute(spans, axis, pairs)
        spans = jnp.where(bit == 0, jnp.concatenate([spans, other]), jnp.concatenate([other, spans]))
        stride *= 2
    return spans


def sum_columns(col_part):
    return lax.psum_scatter(col_part, "row", scatter_dimension=1, tiled=True)


def hypercube_sum(value, axes):
    for axis in axes:
        size = lax.axis_size(axis)
        if size & (size - 1):
            value = lax.psum(value, axis)
            continue
        stride = 1
        while stride < size:
            pairs = [(index, index ^ stride) for index in range(size)]
            value = value + lax.ppermute(value, axis, pairs)
            stride *= 2
    return value


def radix_sum(value, axes, radix=4):
    for axis in axes:
        size = lax.axis_size(axis)
        stride = 1
        while stride < size:
            width = radix if size % (stride * radix) == 0 else 2
            position = lax.axis_index(axis) // stride % width
            received = [value]
            for distance in range(1, width):
                pairs = []
                for index in range(size):
                    member = index // stride % width
                    partner = index + ((member ^ distance) - member) * stride
                    pairs.append((index, partner))
                received.append(lax.ppermute(value, axis, pairs))
            stacked = jnp.stack(received)
            ordered = [
                lax.dynamic_index_in_dim(stacked, position ^ member, 0, keepdims=False)
                for member in range(width)
            ]
            while len(ordered) > 1:
                ordered = [ordered[n] + ordered[n + 1] for n in range(0, len(ordered), 2)]
            value = ordered[0]
            stride *= width
    return value


def exchange_rounds(axes):
    rounds = []
    for axis in axes:
        size = lax.axis_size(axis)
        stride = 1
        while stride < size:
            rounds.append((axis, stride, size))
            stride *= 2
    return rounds


def halving_sum(value, axes):
    shape = value.shape
    flat = value.reshape(-1)
    done = []
    for axis, stride, size in exchange_rounds(axes):
        bit = lax.axis_index(axis) // stride % 2
        halves = flat.reshape(2, -1)
        keep = lax.dynamic_index_in_dim(halves, bit, 0, keepdims=False)
        give = lax.dynamic_index_in_dim(halves, 1 - bit, 0, keepdims=False)
        pairs = [(index, index ^ stride) for index in range(size)]
        flat = keep + lax.ppermute(give, axis, pairs)
        done.append((axis, stride, size, bit))
    for axis, stride, size, bit in reversed(done):
        pairs = [(index, index ^ stride) for index in range(size)]
        other = lax.ppermute(flat, axis, pairs)
        first = jnp.where(bit == 0, flat, other)
        second = jnp.where(bit == 0, other, flat)
        flat = jnp.concatenate([first, second])
    return flat.reshape(shape)


def inverse_factors(gram_blocks):
    factors = jnp.linalg.cholesky(gram_blocks)
    identity = jnp.broadcast_to(jnp.eye(gram_blocks.shape[1], dtype=gram_blocks.dtype), gram_blocks.shape)
    return jax.scipy.linalg.solve_triangular(factors, identity, lower=True)


def shards(probe_block, prior_blocks, self_relatedness, tile_values, tile_index):
    col_count = lax.axis_size("col")
    block_count = prior_blocks.shape[0] + 1
    depth = probe_block.shape[0]
    highest = lax.Precision.HIGHEST
    basis = jnp.concatenate([prior_blocks, probe_block[None]], axis=0)
    flat_basis = basis.reshape(block_count * depth, basis.shape[2])
    wide_basis = flat_basis.astype(jnp.float32)
    gram_local = jnp.dot(flat_basis, flat_basis.T, preferred_element_type=jnp.float32)
    pairs = [(b, e) for b in range(block_count) for e in range(b + 1)]
    lower_local = jnp.stack(
        [gram_local[b * depth:(b + 1) * depth, e * depth:(e + 1) * depth] for b, e in pairs]
    )
    lower = halving_sum(lower_local, ("col", "row"))
    row_probes = lax.all_gather(probe_block, "col", axis=1, tiled=True)
    col_probes = gather_spans(probe_block, "row")
    lower, row_probes, col_probes = lax.optimization_barrier((lower, row_probes, col_probes))
    gram = {pair: lower[n] for n, pair in enumerate(pairs)}
    inverses = inverse_factors(jnp.stack([gram[(b, b)] for b in range(block_count)]))
    row_part, col_part = tile_products(tile_values, tile_index, row_probes, col_probes, col_count)
    row_total = sum_rows(row_part)
    col_total = sum_columns(col_part)
    row_total, col_total, inverses = lax.optimization_barrier((row_total, col_total, inverses))
    product = self_relatedness[None, :] * probe_block.astype(jnp.float32) + row_total + col_total
    along_local = jnp.dot(wide_basis, product.T, precision=highest)
    along = radix_sum(along_local, ("col", "row"))
    solved = []
    for block_number in range(block_count):
        target = along[block_number * depth:(block_number + 1) * depth]
        for earlier in range(block_number):
            target = target - jnp.dot(gram[(block_number, earlier)], solved[earlier], precision=highest)
        inverse = inverses[block_number]
        half = jnp.dot(inverse, target, precision=highest)
        solved.append(jnp.dot(inverse.T, half, precision=highest))
    coefficients = jnp.concatenate(solved, axis=0)
    current = product - jnp.dot(coefficients.T, wide_basis, precision=highest)
    return (current, jnp.stack(solved))


def solution(mesh):
    in_specs = (
        P(None, ("row", "col")),
        P(None, None, ("row", "col")),
        P(("row", "col")),
        P(("row", "col"), None, None),
        P(("row", "col"), None),
    )
    out_specs = (P(None, ("row", "col")), P())
    return jax.shard_map(shards, mesh=mesh, in_specs=in_specs, out_specs=out_specs, check_vma=False)
```

```python
import jax
import jax.numpy as jnp
from jax import lax
from jax.sharding import PartitionSpec as P


def tile_products(tile_values, tile_index, row_probes, col_probes, col_count):
    tile_width = tile_values.shape[1]
    row_spans = row_probes.shape[1] // tile_width
    col_spans = col_probes.shape[1] // tile_width
    forwards, mirrors, row_spans_of, col_spans_of = [], [], [], []
    for slot_index in range(tile_values.shape[0]):
        current_tile = tile_values[slot_index]
        live = tile_index[slot_index, 2] > 0
        row_span = tile_index[slot_index, 0] % col_count
        col_span = tile_index[slot_index, 1] // col_count
        right = lax.dynamic_slice_in_dim(col_probes, col_span * tile_width, tile_width, 1)
        left = lax.dynamic_slice_in_dim(row_probes, row_span * tile_width, tile_width, 1)
        forward = lax.dot_general(
            right, current_tile, (((1,), (1,)), ((), ())), preferred_element_type=jnp.float32
        )
        mirror = jnp.dot(left, current_tile, preferred_element_type=jnp.float32)
        forwards.append(forward)
        mirrors.append(mirror)
        row_spans_of.append(jnp.where(live, row_span, -1))
        col_spans_of.append(jnp.where(live, col_span, -1))
    row_part = jnp.stack(spread_spans(forwards, row_spans_of, row_spans))
    col_part = jnp.concatenate(spread_spans(mirrors, col_spans_of, col_spans), axis=1)
    return row_part, col_part


def spread_spans(terms, spans_of, span_count):
    pieces = []
    for span in range(span_count):
        piece = None
        for term, span_of in zip(terms, spans_of):
            part = jnp.where(span_of == span, term, 0.0)
            piece = part if piece is None else piece + part
        pieces.append(piece)
    return pieces


def sum_rows(row_part):
    size = lax.axis_size("col")
    if size & (size - 1):
        flat = jnp.concatenate(list(row_part), axis=1)
        return lax.psum_scatter(flat, "col", scatter_dimension=1, tiled=True)
    stride = 1
    while stride < size:
        bit = lax.axis_index("col") // stride % 2
        grouped = row_part.reshape(row_part.shape[0] // 2, 2, *row_part.shape[1:])
        keep = lax.dynamic_index_in_dim(grouped, bit, 1, keepdims=False)
        give = lax.dynamic_index_in_dim(grouped, 1 - bit, 1, keepdims=False)
        pairs = [(index, index ^ stride) for index in range(size)]
        row_part = keep + lax.ppermute(give, "col", pairs)
        stride *= 2
    return row_part[0]


def sum_columns(col_part):
    return lax.psum_scatter(col_part, "row", scatter_dimension=1, tiled=True)


def hypercube_sum(value, axes):
    for axis in axes:
        size = lax.axis_size(axis)
        if size & (size - 1):
            value = lax.psum(value, axis)
            continue
        stride = 1
        while stride < size:
            pairs = [(index, index ^ stride) for index in range(size)]
            value = value + lax.ppermute(value, axis, pairs)
            stride *= 2
    return value


def radix_sum(value, axes, radix=4):
    for axis in axes:
        size = lax.axis_size(axis)
        stride = 1
        while stride < size:
            width = radix if size % (stride * radix) == 0 else 2
            position = lax.axis_index(axis) // stride % width
            received = [value]
            for distance in range(1, width):
                pairs = []
                for index in range(size):
                    member = index // stride % width
                    partner = index + ((member ^ distance) - member) * stride
                    pairs.append((index, partner))
                received.append(lax.ppermute(value, axis, pairs))
            stacked = jnp.stack(received)
            ordered = [
                lax.dynamic_index_in_dim(stacked, position ^ member, 0, keepdims=False)
                for member in range(width)
            ]
            while len(ordered) > 1:
                ordered = [ordered[n] + ordered[n + 1] for n in range(0, len(ordered), 2)]
            value = ordered[0]
            stride *= width
    return value


def exchange_rounds(axes):
    rounds = []
    for axis in axes:
        size = lax.axis_size(axis)
        stride = 1
        while stride < size:
            rounds.append((axis, stride, size))
            stride *= 2
    return rounds


def halving_sum(value, axes):
    shape = value.shape
    flat = value.reshape(-1)
    done = []
    for axis, stride, size in exchange_rounds(axes):
        bit = lax.axis_index(axis) // stride % 2
        halves = flat.reshape(2, -1)
        keep = lax.dynamic_index_in_dim(halves, bit, 0, keepdims=False)
        give = lax.dynamic_index_in_dim(halves, 1 - bit, 0, keepdims=False)
        pairs = [(index, index ^ stride) for index in range(size)]
        flat = keep + lax.ppermute(give, axis, pairs)
        done.append((axis, stride, size, bit))
    for axis, stride, size, bit in reversed(done):
        pairs = [(index, index ^ stride) for index in range(size)]
        other = lax.ppermute(flat, axis, pairs)
        first = jnp.where(bit == 0, flat, other)
        second = jnp.where(bit == 0, other, flat)
        flat = jnp.concatenate([first, second])
    return flat.reshape(shape)


def inverse_factors(factors):
    identity = jnp.broadcast_to(jnp.eye(factors.shape[1], dtype=factors.dtype), factors.shape)
    return jax.scipy.linalg.solve_triangular(factors, identity, lower=True)


def shards(probe_block, prior_blocks, self_relatedness, tile_values, tile_index):
    col_count = lax.axis_size("col")
    block_count = prior_blocks.shape[0] + 1
    depth = probe_block.shape[0]
    highest = lax.Precision.HIGHEST
    basis = jnp.concatenate([prior_blocks, probe_block[None]], axis=0)
    flat_basis = basis.reshape(block_count * depth, basis.shape[2])
    wide_basis = flat_basis.astype(jnp.float32)
    gram_local = jnp.dot(flat_basis, flat_basis.T, preferred_element_type=jnp.float32)
    pairs = [(b, e) for b in range(block_count) for e in range(b + 1)]
    lower_local = jnp.stack(
        [gram_local[b * depth:(b + 1) * depth, e * depth:(e + 1) * depth] for b, e in pairs]
    )
    lower = halving_sum(lower_local, ("col", "row"))
    row_probes = lax.all_gather(probe_block, "col", axis=1, tiled=True)
    col_probes = lax.all_gather(probe_block, "row", axis=1, tiled=True)
    gram = {pair: lower[n] for n, pair in enumerate(pairs)}
    factors = jnp.linalg.cholesky(jnp.stack([gram[(b, b)] for b in range(block_count)]))
    factors, row_probes, col_probes = lax.optimization_barrier((factors, row_probes, col_probes))
    inverses = inverse_factors(factors)
    row_part, col_part = tile_products(tile_values, tile_index, row_probes, col_probes, col_count)
    row_total = sum_rows(row_part)
    col_total = sum_columns(col_part)
    row_total, col_total, inverses = lax.optimization_barrier((row_total, col_total, inverses))
    product = self_relatedness[None, :] * probe_block.astype(jnp.float32) + row_total + col_total
    along_local = jnp.dot(wide_basis, product.T, precision=highest)
    along = radix_sum(along_local, ("col", "row"))
    solved = []
    for block_number in range(block_count):
        target = along[block_number * depth:(block_number + 1) * depth]
        for earlier in range(block_number):
            target = target - jnp.dot(gram[(block_number, earlier)], solved[earlier], precision=highest)
        inverse = inverses[block_number]
        half = jnp.dot(inverse, target, precision=highest)
        solved.append(jnp.dot(inverse.T, half, precision=highest))
    coefficients = jnp.concatenate(solved, axis=0)
    current = product - jnp.dot(coefficients.T, wide_basis, precision=highest)
    return (current, jnp.stack(solved))


def solution(mesh):
    in_specs = (
        P(None, ("row", "col")),
        P(None, None, ("row", "col")),
        P(("row", "col")),
        P(("row", "col"), None, None),
        P(("row", "col"), None),
    )
    out_specs = (P(None, ("row", "col")), P())
    return jax.shard_map(shards, mesh=mesh, in_specs=in_specs, out_specs=out_specs, check_vma=False)
```

```python
import jax
import jax.numpy as jnp
from jax import lax
from jax.sharding import PartitionSpec as P


def tile_products(tile_values, tile_index, row_probes, col_probes, col_count):
    tile_width = tile_values.shape[1]
    row_spans = row_probes.shape[1] // tile_width
    col_spans = col_probes.shape[1] // tile_width
    live = [tile_index[slot, 2] > 0 for slot in range(tile_values.shape[0])]
    row_of = [tile_index[slot, 0] % col_count for slot in range(tile_values.shape[0])]
    col_of = [tile_index[slot, 1] // col_count for slot in range(tile_values.shape[0])]
    forwards = []
    for slot in range(tile_values.shape[0]):
        right = lax.dynamic_slice_in_dim(col_probes, col_of[slot] * tile_width, tile_width, 1)
        forwards.append(lax.dot_general(
            right, tile_values[slot], (((1,), (1,)), ((), ())), preferred_element_type=jnp.float32
        ))
    row_part = jnp.stack(spread_spans(
        forwards, [jnp.where(l, r, -1) for l, r in zip(live, row_of)], row_spans
    ))
    row_part, (tile_values, row_probes) = sum_rows(row_part, (tile_values, row_probes))
    mirrors = []
    for slot in range(tile_values.shape[0]):
        left = lax.dynamic_slice_in_dim(row_probes, row_of[slot] * tile_width, tile_width, 1)
        mirrors.append(jnp.dot(left, tile_values[slot], preferred_element_type=jnp.float32))
    col_part = jnp.concatenate(spread_spans(
        mirrors, [jnp.where(l, c, -1) for l, c in zip(live, col_of)], col_spans
    ), axis=1)
    return row_part, col_part


def spread_spans(terms, spans_of, span_count):
    pieces = []
    for span in range(span_count):
        piece = None
        for term, span_of in zip(terms, spans_of):
            part = jnp.where(span_of == span, term, 0.0)
            piece = part if piece is None else piece + part
        pieces.append(piece)
    return pieces


def sum_rows(row_part, riders):
    size = lax.axis_size("col")
    if size & (size - 1):
        flat = jnp.concatenate(list(row_part), axis=1)
        return lax.psum_scatter(flat, "col", scatter_dimension=1, tiled=True), riders
    stride = 1
    while stride < size:
        bit = lax.axis_index("col") // stride % 2
        grouped = row_part.reshape(row_part.shape[0] // 2, 2, *row_part.shape[1:])
        keep = lax.dynamic_index_in_dim(grouped, bit, 1, keepdims=False)
        give = lax.dynamic_index_in_dim(grouped, 1 - bit, 1, keepdims=False)
        pairs = [(index, index ^ stride) for index in range(size)]
        row_part = keep + lax.ppermute(give, "col", pairs)
        if stride == 1:
            row_part, riders = lax.optimization_barrier((row_part, riders))
        stride *= 2
    return row_part[0], riders


def sum_columns(col_part):
    return lax.psum_scatter(col_part, "row", scatter_dimension=1, tiled=True)


def hypercube_sum(value, axes):
    for axis in axes:
        size = lax.axis_size(axis)
        if size & (size - 1):
            value = lax.psum(value, axis)
            continue
        stride = 1
        while stride < size:
            pairs = [(index, index ^ stride) for index in range(size)]
            value = value + lax.ppermute(value, axis, pairs)
            stride *= 2
    return value


def radix_sum(value, axes, radix=4):
    for axis in axes:
        size = lax.axis_size(axis)
        stride = 1
        while stride < size:
            width = radix if size % (stride * radix) == 0 else 2
            position = lax.axis_index(axis) // stride % width
            received = [value]
            for distance in range(1, width):
                pairs = []
                for index in range(size):
                    member = index // stride % width
                    partner = index + ((member ^ distance) - member) * stride
                    pairs.append((index, partner))
                received.append(lax.ppermute(value, axis, pairs))
            stacked = jnp.stack(received)
            ordered = [
                lax.dynamic_index_in_dim(stacked, position ^ member, 0, keepdims=False)
                for member in range(width)
            ]
            while len(ordered) > 1:
                ordered = [ordered[n] + ordered[n + 1] for n in range(0, len(ordered), 2)]
            value = ordered[0]
            stride *= width
    return value


def exchange_rounds(axes):
    rounds = []
    for axis in axes:
        size = lax.axis_size(axis)
        stride = 1
        while stride < size:
            rounds.append((axis, stride, size))
            stride *= 2
    return rounds


def halving_sum(value, axes):
    shape = value.shape
    flat = value.reshape(-1)
    done = []
    for axis, stride, size in exchange_rounds(axes):
        bit = lax.axis_index(axis) // stride % 2
        halves = flat.reshape(2, -1)
        keep = lax.dynamic_index_in_dim(halves, bit, 0, keepdims=False)
        give = lax.dynamic_index_in_dim(halves, 1 - bit, 0, keepdims=False)
        pairs = [(index, index ^ stride) for index in range(size)]
        flat = keep + lax.ppermute(give, axis, pairs)
        done.append((axis, stride, size, bit))
    for axis, stride, size, bit in reversed(done):
        pairs = [(index, index ^ stride) for index in range(size)]
        other = lax.ppermute(flat, axis, pairs)
        first = jnp.where(bit == 0, flat, other)
        second = jnp.where(bit == 0, other, flat)
        flat = jnp.concatenate([first, second])
    return flat.reshape(shape)


def inverse_factors(gram_blocks):
    factors = jnp.linalg.cholesky(gram_blocks)
    identity = jnp.broadcast_to(jnp.eye(gram_blocks.shape[1], dtype=gram_blocks.dtype), gram_blocks.shape)
    return jax.scipy.linalg.solve_triangular(factors, identity, lower=True)


def shards(probe_block, prior_blocks, self_relatedness, tile_values, tile_index):
    col_count = lax.axis_size("col")
    block_count = prior_blocks.shape[0] + 1
    depth = probe_block.shape[0]
    highest = lax.Precision.HIGHEST
    basis = jnp.concatenate([prior_blocks, probe_block[None]], axis=0)
    flat_basis = basis.reshape(block_count * depth, basis.shape[2])
    wide_basis = flat_basis.astype(jnp.float32)
    gram_local = jnp.dot(flat_basis, flat_basis.T, preferred_element_type=jnp.float32)
    pairs = [(b, e) for b in range(block_count) for e in range(b + 1)]
    lower_local = jnp.stack(
        [gram_local[b * depth:(b + 1) * depth, e * depth:(e + 1) * depth] for b, e in pairs]
    )
    lower = halving_sum(lower_local, ("col", "row"))
    row_probes = lax.all_gather(probe_block, "col", axis=1, tiled=True)
    col_probes = lax.all_gather(probe_block, "row", axis=1, tiled=True)
    lower, row_probes, col_probes = lax.optimization_barrier((lower, row_probes, col_probes))
    gram = {pair: lower[n] for n, pair in enumerate(pairs)}
    inverses = inverse_factors(jnp.stack([gram[(b, b)] for b in range(block_count)]))
    row_part, col_part = tile_products(tile_values, tile_index, row_probes, col_probes, col_count)
    row_total = row_part
    col_total = sum_columns(col_part)
    row_total, col_total, inverses = lax.optimization_barrier((row_total, col_total, inverses))
    product = self_relatedness[None, :] * probe_block.astype(jnp.float32) + row_total + col_total
    along_local = jnp.dot(wide_basis, product.T, precision=highest)
    along = radix_sum(along_local, ("col", "row"))
    solved = []
    for block_number in range(block_count):
        target = along[block_number * depth:(block_number + 1) * depth]
        for earlier in range(block_number):
            target = target - jnp.dot(gram[(block_number, earlier)], solved[earlier], precision=highest)
        inverse = inverses[block_number]
        half = jnp.dot(inverse, target, precision=highest)
        solved.append(jnp.dot(inverse.T, half, precision=highest))
    coefficients = jnp.concatenate(solved, axis=0)
    current = product - jnp.dot(coefficients.T, wide_basis, precision=highest)
    return (current, jnp.stack(solved))


def solution(mesh):
    in_specs = (
        P(None, ("row", "col")),
        P(None, None, ("row", "col")),
        P(("row", "col")),
        P(("row", "col"), None, None),
        P(("row", "col"), None),
    )
    out_specs = (P(None, ("row", "col")), P())
    return jax.shard_map(shards, mesh=mesh, in_specs=in_specs, out_specs=out_specs, check_vma=False)
```

```python
import jax
import jax.numpy as jnp
from jax import lax
from jax.sharding import PartitionSpec as P


def tile_products(tile_values, tile_index, row_probes, col_probes, col_count):
    tile_width = tile_values.shape[1]
    row_spans = row_probes.shape[1] // tile_width
    col_spans = col_probes.shape[1] // tile_width
    forwards, mirrors, row_spans_of, col_spans_of = [], [], [], []
    for slot_index in range(tile_values.shape[0]):
        current_tile = tile_values[slot_index]
        live = tile_index[slot_index, 2] > 0
        row_span = tile_index[slot_index, 0] % col_count
        col_span = tile_index[slot_index, 1] // col_count
        right = lax.dynamic_slice_in_dim(col_probes, col_span * tile_width, tile_width, 1)
        left = lax.dynamic_slice_in_dim(row_probes, row_span * tile_width, tile_width, 1)
        forward = lax.dot_general(
            right, current_tile, (((1,), (1,)), ((), ())), preferred_element_type=jnp.float32
        )
        mirror = jnp.dot(left, current_tile, preferred_element_type=jnp.float32)
        forwards.append(forward)
        mirrors.append(mirror)
        row_spans_of.append(jnp.where(live, row_span, -1))
        col_spans_of.append(jnp.where(live, col_span, -1))
    row_part = jnp.stack(spread_spans(forwards, row_spans_of, row_spans))
    col_part = jnp.concatenate(spread_spans(mirrors, col_spans_of, col_spans), axis=1)
    return row_part, col_part


def spread_spans(terms, spans_of, span_count):
    pieces = []
    for span in range(span_count):
        piece = None
        for term, span_of in zip(terms, spans_of):
            part = jnp.where(span_of == span, term, 0.0)
            piece = part if piece is None else piece + part
        pieces.append(piece)
    return pieces


def sum_rows(row_part):
    size = lax.axis_size("col")
    if size & (size - 1):
        flat = jnp.concatenate(list(row_part), axis=1)
        return lax.psum_scatter(flat, "col", scatter_dimension=1, tiled=True)
    stride = 1
    while stride < size:
        bit = lax.axis_index("col") // stride % 2
        grouped = row_part.reshape(row_part.shape[0] // 2, 2, *row_part.shape[1:])
        keep = lax.dynamic_index_in_dim(grouped, bit, 1, keepdims=False)
        give = lax.dynamic_index_in_dim(grouped, 1 - bit, 1, keepdims=False)
        pairs = [(index, index ^ stride) for index in range(size)]
        row_part = keep + lax.ppermute(give, "col", pairs)
        stride *= 2
    return row_part[0]


def sum_columns(col_part):
    return lax.psum_scatter(col_part, "row", scatter_dimension=1, tiled=True)


def hypercube_sum(value, axes):
    for axis in axes:
        size = lax.axis_size(axis)
        if size & (size - 1):
            value = lax.psum(value, axis)
            continue
        stride = 1
        while stride < size:
            pairs = [(index, index ^ stride) for index in range(size)]
            value = value + lax.ppermute(value, axis, pairs)
            stride *= 2
    return value


def radix_sum(value, axes, radix=4):
    for axis in axes:
        size = lax.axis_size(axis)
        stride = 1
        while stride < size:
            width = radix if size % (stride * radix) == 0 else 2
            position = lax.axis_index(axis) // stride % width
            received = [value]
            for distance in range(1, width):
                pairs = []
                for index in range(size):
                    member = index // stride % width
                    partner = index + ((member ^ distance) - member) * stride
                    pairs.append((index, partner))
                received.append(lax.ppermute(value, axis, pairs))
            stacked = jnp.stack(received)
            ordered = [
                lax.dynamic_index_in_dim(stacked, position ^ member, 0, keepdims=False)
                for member in range(width)
            ]
            while len(ordered) > 1:
                ordered = [ordered[n] + ordered[n + 1] for n in range(0, len(ordered), 2)]
            value = ordered[0]
            stride *= width
    return value


def exchange_rounds(axes):
    rounds = []
    for axis in axes:
        size = lax.axis_size(axis)
        stride = 1
        while stride < size:
            rounds.append((axis, stride, size))
            stride *= 2
    return rounds


def halving_sum(value, axes):
    shape = value.shape
    flat = value.reshape(-1)
    done = []
    for axis, stride, size in exchange_rounds(axes):
        bit = lax.axis_index(axis) // stride % 2
        halves = flat.reshape(2, -1)
        keep = lax.dynamic_index_in_dim(halves, bit, 0, keepdims=False)
        give = lax.dynamic_index_in_dim(halves, 1 - bit, 0, keepdims=False)
        pairs = [(index, index ^ stride) for index in range(size)]
        flat = keep + lax.ppermute(give, axis, pairs)
        done.append((axis, stride, size, bit))
    for axis, stride, size, bit in reversed(done):
        pairs = [(index, index ^ stride) for index in range(size)]
        other = lax.ppermute(flat, axis, pairs)
        first = jnp.where(bit == 0, flat, other)
        second = jnp.where(bit == 0, other, flat)
        flat = jnp.concatenate([first, second])
    return flat.reshape(shape)


def inverse_factors(gram_blocks):
    factors = jnp.linalg.cholesky(gram_blocks)
    identity = jnp.broadcast_to(jnp.eye(gram_blocks.shape[1], dtype=gram_blocks.dtype), gram_blocks.shape)
    return jax.scipy.linalg.solve_triangular(factors, identity, lower=True)


def shards(probe_block, prior_blocks, self_relatedness, tile_values, tile_index):
    col_count = lax.axis_size("col")
    block_count = prior_blocks.shape[0] + 1
    depth = probe_block.shape[0]
    highest = lax.Precision.HIGHEST
    basis = jnp.concatenate([prior_blocks, probe_block[None]], axis=0)
    flat_basis = basis.reshape(block_count * depth, basis.shape[2])
    wide_basis = flat_basis.astype(jnp.float32)
    gram_local = jnp.dot(flat_basis, flat_basis.T, preferred_element_type=jnp.float32)
    def block(b, e):
        return gram_local[b * depth:(b + 1) * depth, e * depth:(e + 1) * depth]

    diagonal = halving_sum(jnp.stack([block(b, b) for b in range(block_count)]), ("col", "row"))
    pairs = [(b, e) for b in range(block_count) for e in range(b)]
    off_diagonal = halving_sum(jnp.stack([block(b, e) for b, e in pairs]), ("col", "row"))
    row_probes = lax.all_gather(probe_block, "col", axis=1, tiled=True)
    col_probes = lax.all_gather(probe_block, "row", axis=1, tiled=True)
    inverses = inverse_factors(diagonal)
    inverses, row_probes, col_probes = lax.optimization_barrier((inverses, row_probes, col_probes))
    row_part, col_part = tile_products(tile_values, tile_index, row_probes, col_probes, col_count)
    row_total = sum_rows(row_part)
    col_total = sum_columns(col_part)
    row_total, col_total, off_diagonal = lax.optimization_barrier((row_total, col_total, off_diagonal))
    gram = {pair: off_diagonal[n] for n, pair in enumerate(pairs)}
    product = self_relatedness[None, :] * probe_block.astype(jnp.float32) + row_total + col_total
    along_local = jnp.dot(wide_basis, product.T, precision=highest)
    along = radix_sum(along_local, ("col", "row"))
    solved = []
    for block_number in range(block_count):
        target = along[block_number * depth:(block_number + 1) * depth]
        for earlier in range(block_number):
            target = target - jnp.dot(gram[(block_number, earlier)], solved[earlier], precision=highest)
        inverse = inverses[block_number]
        half = jnp.dot(inverse, target, precision=highest)
        solved.append(jnp.dot(inverse.T, half, precision=highest))
    coefficients = jnp.concatenate(solved, axis=0)
    current = product - jnp.dot(coefficients.T, wide_basis, precision=highest)
    return (current, jnp.stack(solved))


def solution(mesh):
    in_specs = (
        P(None, ("row", "col")),
        P(None, None, ("row", "col")),
        P(("row", "col")),
        P(("row", "col"), None, None),
        P(("row", "col"), None),
    )
    out_specs = (P(None, ("row", "col")), P())
    return jax.shard_map(shards, mesh=mesh, in_specs=in_specs, out_specs=out_specs, check_vma=False)
```

```python
import jax
import jax.numpy as jnp
from jax import lax
from jax.sharding import PartitionSpec as P


def tile_products(tile_values, tile_index, row_probes, col_probes, col_count):
    tile_width = tile_values.shape[1]
    row_spans = row_probes.shape[1] // tile_width
    col_spans = col_probes.shape[1] // tile_width
    forwards, mirrors, row_spans_of, col_spans_of = [], [], [], []
    for slot_index in range(tile_values.shape[0]):
        current_tile = tile_values[slot_index]
        live = tile_index[slot_index, 2] > 0
        row_span = tile_index[slot_index, 0] % col_count
        col_span = tile_index[slot_index, 1] // col_count
        right = lax.dynamic_slice_in_dim(col_probes, col_span * tile_width, tile_width, 1)
        left = lax.dynamic_slice_in_dim(row_probes, row_span * tile_width, tile_width, 1)
        forward = lax.dot_general(
            right, current_tile, (((1,), (1,)), ((), ())), preferred_element_type=jnp.float32
        )
        mirror = jnp.dot(left, current_tile, preferred_element_type=jnp.float32)
        forwards.append(forward)
        mirrors.append(mirror)
        row_spans_of.append(jnp.where(live, row_span, -1))
        col_spans_of.append(jnp.where(live, col_span, -1))
    row_part = jnp.stack(spread_spans(forwards, row_spans_of, row_spans))
    col_part = jnp.concatenate(spread_spans(mirrors, col_spans_of, col_spans), axis=1)
    return row_part, col_part


def spread_spans(terms, spans_of, span_count):
    pieces = []
    for span in range(span_count):
        piece = None
        for term, span_of in zip(terms, spans_of):
            part = jnp.where(span_of == span, term, 0.0)
            piece = part if piece is None else piece + part
        pieces.append(piece)
    return pieces


def sum_rows(row_part):
    size = lax.axis_size("col")
    if size & (size - 1):
        flat = jnp.concatenate(list(row_part), axis=1)
        return lax.psum_scatter(flat, "col", scatter_dimension=1, tiled=True)
    stride = 1
    while stride < size:
        bit = lax.axis_index("col") // stride % 2
        grouped = row_part.reshape(row_part.shape[0] // 2, 2, *row_part.shape[1:])
        keep = lax.dynamic_index_in_dim(grouped, bit, 1, keepdims=False)
        give = lax.dynamic_index_in_dim(grouped, 1 - bit, 1, keepdims=False)
        pairs = [(index, index ^ stride) for index in range(size)]
        row_part = keep + lax.ppermute(give, "col", pairs)
        stride *= 2
    return row_part[0]


def sum_columns(col_part):
    return lax.psum_scatter(col_part, "row", scatter_dimension=1, tiled=True)


def hypercube_sum(value, axes):
    for axis in axes:
        size = lax.axis_size(axis)
        if size & (size - 1):
            value = lax.psum(value, axis)
            continue
        stride = 1
        while stride < size:
            pairs = [(index, index ^ stride) for index in range(size)]
            value = value + lax.ppermute(value, axis, pairs)
            stride *= 2
    return value


def radix_sum(value, axes, radix=4):
    for axis in axes:
        size = lax.axis_size(axis)
        stride = 1
        while stride < size:
            width = radix if size % (stride * radix) == 0 else 2
            position = lax.axis_index(axis) // stride % width
            received = [value]
            for distance in range(1, width):
                pairs = []
                for index in range(size):
                    member = index // stride % width
                    partner = index + ((member ^ distance) - member) * stride
                    pairs.append((index, partner))
                received.append(lax.ppermute(value, axis, pairs))
            stacked = jnp.stack(received)
            ordered = [
                lax.dynamic_index_in_dim(stacked, position ^ member, 0, keepdims=False)
                for member in range(width)
            ]
            while len(ordered) > 1:
                ordered = [ordered[n] + ordered[n + 1] for n in range(0, len(ordered), 2)]
            value = ordered[0]
            stride *= width
    return value


def exchange_rounds(axes):
    rounds = []
    for axis in axes:
        size = lax.axis_size(axis)
        stride = 1
        while stride < size:
            rounds.append((axis, stride, size))
            stride *= 2
    return rounds


def halving_sum(value, axes):
    shape = value.shape
    flat = value.reshape(-1)
    done = []
    for axis, stride, size in exchange_rounds(axes):
        bit = lax.axis_index(axis) // stride % 2
        halves = flat.reshape(2, -1)
        keep = lax.dynamic_index_in_dim(halves, bit, 0, keepdims=False)
        give = lax.dynamic_index_in_dim(halves, 1 - bit, 0, keepdims=False)
        pairs = [(index, index ^ stride) for index in range(size)]
        flat = keep + lax.ppermute(give, axis, pairs)
        done.append((axis, stride, size, bit))
    for axis, stride, size, bit in reversed(done):
        pairs = [(index, index ^ stride) for index in range(size)]
        other = lax.ppermute(flat, axis, pairs)
        first = jnp.where(bit == 0, flat, other)
        second = jnp.where(bit == 0, other, flat)
        flat = jnp.concatenate([first, second])
    return flat.reshape(shape)


def inverse_factors(gram_blocks):
    factors = jnp.linalg.cholesky(gram_blocks)
    identity = jnp.broadcast_to(jnp.eye(gram_blocks.shape[1], dtype=gram_blocks.dtype), gram_blocks.shape)
    return jax.scipy.linalg.solve_triangular(factors, identity, lower=True)


def shards(probe_block, prior_blocks, self_relatedness, tile_values, tile_index):
    col_count = lax.axis_size("col")
    block_count = prior_blocks.shape[0] + 1
    depth = probe_block.shape[0]
    highest = lax.Precision.HIGHEST
    basis = jnp.concatenate([prior_blocks, probe_block[None]], axis=0)
    flat_basis = basis.reshape(block_count * depth, basis.shape[2])
    wide_basis = flat_basis.astype(jnp.float32)
    gram_local = jnp.dot(flat_basis, flat_basis.T, preferred_element_type=jnp.float32)
    pairs = [(b, e) for b in range(block_count) for e in range(b + 1)]
    lower_local = jnp.stack(
        [gram_local[b * depth:(b + 1) * depth, e * depth:(e + 1) * depth] for b, e in pairs]
    )
    lower = halving_sum(lower_local, ("col", "row"))
    row_probes = lax.all_gather(probe_block, "col", axis=1, tiled=True)
    col_probes = lax.all_gather(probe_block, "row", axis=1, tiled=True)
    lower, row_probes, col_probes = lax.optimization_barrier((lower, row_probes, col_probes))
    gram = {pair: lower[n] for n, pair in enumerate(pairs)}
    factors = jnp.linalg.cholesky(jnp.stack([gram[(b, b)] for b in range(block_count)]))
    row_part, col_part = tile_products(tile_values, tile_index, row_probes, col_probes, col_count)
    row_total = sum_rows(row_part)
    col_total = sum_columns(col_part)
    row_total, col_total, factors = lax.optimization_barrier((row_total, col_total, factors))
    product = self_relatedness[None, :] * probe_block.astype(jnp.float32) + row_total + col_total
    along_local = jnp.dot(wide_basis, product.T, precision=highest)
    along = radix_sum(along_local, ("col", "row"))
    solved = []
    for block_number in range(block_count):
        target = along[block_number * depth:(block_number + 1) * depth]
        for earlier in range(block_number):
            target = target - jnp.dot(gram[(block_number, earlier)], solved[earlier], precision=highest)
        solved.append(jax.scipy.linalg.cho_solve((factors[block_number], True), target))
    coefficients = jnp.concatenate(solved, axis=0)
    current = product - jnp.dot(coefficients.T, wide_basis, precision=highest)
    return (current, jnp.stack(solved))


def solution(mesh):
    in_specs = (
        P(None, ("row", "col")),
        P(None, None, ("row", "col")),
        P(("row", "col")),
        P(("row", "col"), None, None),
        P(("row", "col"), None),
    )
    out_specs = (P(None, ("row", "col")), P())
    return jax.shard_map(shards, mesh=mesh, in_specs=in_specs, out_specs=out_specs, check_vma=False)
```

```python
import jax
import jax.numpy as jnp
from jax import lax
from jax.sharding import PartitionSpec as P


def tile_products(tile_values, tile_index, row_probes, col_probes, col_count):
    tile_width = tile_values.shape[1]
    row_spans = row_probes.shape[1] // tile_width
    col_spans = col_probes.shape[1] // tile_width
    forwards, mirrors, row_spans_of, col_spans_of = [], [], [], []
    for slot_index in range(tile_values.shape[0]):
        current_tile = tile_values[slot_index]
        live = tile_index[slot_index, 2] > 0
        row_span = tile_index[slot_index, 0] % col_count
        col_span = tile_index[slot_index, 1] // col_count
        right = lax.dynamic_slice_in_dim(col_probes, col_span * tile_width, tile_width, 1)
        left = lax.dynamic_slice_in_dim(row_probes, row_span * tile_width, tile_width, 1)
        forward = lax.dot_general(
            right, current_tile, (((1,), (1,)), ((), ())), preferred_element_type=jnp.float32
        )
        mirror = jnp.dot(left, current_tile, preferred_element_type=jnp.float32)
        forwards.append(forward)
        mirrors.append(mirror)
        row_spans_of.append(jnp.where(live, row_span, -1))
        col_spans_of.append(jnp.where(live, col_span, -1))
    row_part = jnp.stack(spread_spans(forwards, row_spans_of, row_spans))
    col_part = jnp.concatenate(spread_spans(mirrors, col_spans_of, col_spans), axis=1)
    return row_part, col_part


def spread_spans(terms, spans_of, span_count):
    pieces = []
    for span in range(span_count):
        piece = None
        for term, span_of in zip(terms, spans_of):
            part = jnp.where(span_of == span, term, 0.0)
            piece = part if piece is None else piece + part
        pieces.append(piece)
    return pieces


def sum_rows(row_part):
    size = lax.axis_size("col")
    if size & (size - 1):
        flat = jnp.concatenate(list(row_part), axis=1)
        return lax.psum_scatter(flat, "col", scatter_dimension=1, tiled=True)
    stride = 1
    while stride < size:
        bit = lax.axis_index("col") // stride % 2
        grouped = row_part.reshape(row_part.shape[0] // 2, 2, *row_part.shape[1:])
        keep = lax.dynamic_index_in_dim(grouped, bit, 1, keepdims=False)
        give = lax.dynamic_index_in_dim(grouped, 1 - bit, 1, keepdims=False)
        pairs = [(index, index ^ stride) for index in range(size)]
        row_part = keep + lax.ppermute(give, "col", pairs)
        stride *= 2
    return row_part[0]


def sum_columns(col_part):
    return lax.psum_scatter(col_part, "row", scatter_dimension=1, tiled=True)


def hypercube_sum(value, axes):
    for axis in axes:
        size = lax.axis_size(axis)
        if size & (size - 1):
            value = lax.psum(value, axis)
            continue
        stride = 1
        while stride < size:
            pairs = [(index, index ^ stride) for index in range(size)]
            value = value + lax.ppermute(value, axis, pairs)
            stride *= 2
    return value


def radix_sum(value, axes, radix=4):
    for axis in axes:
        size = lax.axis_size(axis)
        stride = 1
        while stride < size:
            width = radix if size % (stride * radix) == 0 else 2
            position = lax.axis_index(axis) // stride % width
            received = [value]
            for distance in range(1, width):
                pairs = []
                for index in range(size):
                    member = index // stride % width
                    partner = index + ((member ^ distance) - member) * stride
                    pairs.append((index, partner))
                received.append(lax.ppermute(value, axis, pairs))
            stacked = jnp.stack(received)
            ordered = [
                lax.dynamic_index_in_dim(stacked, position ^ member, 0, keepdims=False)
                for member in range(width)
            ]
            while len(ordered) > 1:
                ordered = [ordered[n] + ordered[n + 1] for n in range(0, len(ordered), 2)]
            value = ordered[0]
            stride *= width
    return value


def exchange_rounds(axes):
    rounds = []
    for axis in axes:
        size = lax.axis_size(axis)
        stride = 1
        while stride < size:
            rounds.append((axis, stride, size))
            stride *= 2
    return rounds


def halving_sum(value, axes):
    shape = value.shape
    flat = value.reshape(-1)
    done = []
    for axis, stride, size in exchange_rounds(axes):
        bit = lax.axis_index(axis) // stride % 2
        halves = flat.reshape(2, -1)
        keep = lax.dynamic_index_in_dim(halves, bit, 0, keepdims=False)
        give = lax.dynamic_index_in_dim(halves, 1 - bit, 0, keepdims=False)
        pairs = [(index, index ^ stride) for index in range(size)]
        flat = keep + lax.ppermute(give, axis, pairs)
        done.append((axis, stride, size, bit))
    for axis, stride, size, bit in reversed(done):
        pairs = [(index, index ^ stride) for index in range(size)]
        other = lax.ppermute(flat, axis, pairs)
        first = jnp.where(bit == 0, flat, other)
        second = jnp.where(bit == 0, other, flat)
        flat = jnp.concatenate([first, second])
    return flat.reshape(shape)


def inverse_factors(gram_blocks):
    factors = jnp.linalg.cholesky(gram_blocks)
    identity = jnp.broadcast_to(jnp.eye(gram_blocks.shape[1], dtype=gram_blocks.dtype), gram_blocks.shape)
    return jax.scipy.linalg.solve_triangular(factors, identity, lower=True)


def shards(probe_block, prior_blocks, self_relatedness, tile_values, tile_index):
    col_count = lax.axis_size("col")
    block_count = prior_blocks.shape[0] + 1
    depth = probe_block.shape[0]
    highest = lax.Precision.HIGHEST
    basis = jnp.concatenate([prior_blocks, probe_block[None]], axis=0)
    flat_basis = basis.reshape(block_count * depth, basis.shape[2])
    wide_basis = flat_basis.astype(jnp.float32)
    gram_local = jnp.dot(flat_basis, flat_basis.T, preferred_element_type=jnp.float32)
    pairs = [(b, e) for b in range(block_count) for e in range(b + 1)]
    lower_local = jnp.stack(
        [gram_local[b * depth:(b + 1) * depth, e * depth:(e + 1) * depth] for b, e in pairs]
    )
    lower = halving_sum(lower_local, ("col", "row"))
    row_probes = lax.all_gather(probe_block, "col", axis=1, tiled=True)
    col_probes = lax.all_gather(probe_block, "row", axis=1, tiled=True)
    gram = {pair: lower[n] for n, pair in enumerate(pairs)}
    inverses = inverse_factors(jnp.stack([gram[(b, b)] for b in range(block_count)]))
    row_part, col_part = tile_products(tile_values, tile_index, row_probes, col_probes, col_count)
    row_total = sum_rows(row_part)
    col_total = sum_columns(col_part)
    row_total, col_total, inverses = lax.optimization_barrier((row_total, col_total, inverses))
    product = self_relatedness[None, :] * probe_block.astype(jnp.float32) + row_total + col_total
    along_local = jnp.dot(wide_basis, product.T, precision=highest)
    along = radix_sum(along_local, ("col", "row"))
    solved = []
    for block_number in range(block_count):
        target = along[block_number * depth:(block_number + 1) * depth]
        for earlier in range(block_number):
            target = target - jnp.dot(gram[(block_number, earlier)], solved[earlier], precision=highest)
        inverse = inverses[block_number]
        half = jnp.dot(inverse, target, precision=highest)
        solved.append(jnp.dot(inverse.T, half, precision=highest))
    coefficients = jnp.concatenate(solved, axis=0)
    current = product - jnp.dot(coefficients.T, wide_basis, precision=highest)
    return (current, jnp.stack(solved))


def solution(mesh):
    in_specs = (
        P(None, ("row", "col")),
        P(None, None, ("row", "col")),
        P(("row", "col")),
        P(("row", "col"), None, None),
        P(("row", "col"), None),
    )
    out_specs = (P(None, ("row", "col")), P())
    return jax.shard_map(shards, mesh=mesh, in_specs=in_specs, out_specs=out_specs, check_vma=False)
```

```python
import jax
import jax.numpy as jnp
from jax import lax
from jax.sharding import PartitionSpec as P


def tile_products(tile_values, tile_index, row_probes, col_probes, col_count):
    tile_width = tile_values.shape[1]
    row_spans = row_probes.shape[1] // tile_width
    col_spans = col_probes.shape[1] // tile_width
    forwards, mirrors, row_spans_of, col_spans_of = [], [], [], []
    for slot_index in range(tile_values.shape[0]):
        current_tile = tile_values[slot_index]
        live = tile_index[slot_index, 2] > 0
        row_span = tile_index[slot_index, 0] % col_count
        col_span = tile_index[slot_index, 1] // col_count
        right = lax.dynamic_slice_in_dim(col_probes, col_span * tile_width, tile_width, 1)
        left = lax.dynamic_slice_in_dim(row_probes, row_span * tile_width, tile_width, 1)
        forward = lax.dot_general(
            right, current_tile, (((1,), (1,)), ((), ())), preferred_element_type=jnp.float32
        )
        mirror = jnp.dot(left, current_tile, preferred_element_type=jnp.float32)
        forwards.append(forward)
        mirrors.append(mirror)
        row_spans_of.append(jnp.where(live, row_span, -1))
        col_spans_of.append(jnp.where(live, col_span, -1))
    row_part = jnp.stack(spread_spans(forwards, row_spans_of, row_spans))
    col_part = jnp.concatenate(spread_spans(mirrors, col_spans_of, col_spans), axis=1)
    return row_part, col_part


def spread_spans(terms, spans_of, span_count):
    pieces = []
    for span in range(span_count):
        piece = None
        for term, span_of in zip(terms, spans_of):
            part = jnp.where(span_of == span, term, 0.0)
            piece = part if piece is None else piece + part
        pieces.append(piece)
    return pieces


def sum_rows(row_part):
    size = lax.axis_size("col")
    if size & (size - 1):
        flat = jnp.concatenate(list(row_part), axis=1)
        return lax.psum_scatter(flat, "col", scatter_dimension=1, tiled=True)
    stride = 1
    while stride < size:
        bit = lax.axis_index("col") // stride % 2
        grouped = row_part.reshape(row_part.shape[0] // 2, 2, *row_part.shape[1:])
        keep = lax.dynamic_index_in_dim(grouped, bit, 1, keepdims=False)
        give = lax.dynamic_index_in_dim(grouped, 1 - bit, 1, keepdims=False)
        pairs = [(index, index ^ stride) for index in range(size)]
        row_part = keep + lax.ppermute(give, "col", pairs)
        stride *= 2
    return row_part[0]


def sum_columns(col_part):
    return lax.psum_scatter(col_part, "row", scatter_dimension=1, tiled=True)


def hypercube_sum(value, axes):
    for axis in axes:
        size = lax.axis_size(axis)
        if size & (size - 1):
            value = lax.psum(value, axis)
            continue
        stride = 1
        while stride < size:
            pairs = [(index, index ^ stride) for index in range(size)]
            value = value + lax.ppermute(value, axis, pairs)
            stride *= 2
    return value


def radix_sum(value, axes, radix=4):
    for axis in axes:
        size = lax.axis_size(axis)
        stride = 1
        while stride < size:
            width = radix if size % (stride * radix) == 0 else 2
            position = lax.axis_index(axis) // stride % width
            received = [value]
            for distance in range(1, width):
                pairs = []
                for index in range(size):
                    member = index // stride % width
                    partner = index + ((member ^ distance) - member) * stride
                    pairs.append((index, partner))
                received.append(lax.ppermute(value, axis, pairs))
            stacked = jnp.stack(received)
            ordered = [
                lax.dynamic_index_in_dim(stacked, position ^ member, 0, keepdims=False)
                for member in range(width)
            ]
            while len(ordered) > 1:
                ordered = [ordered[n] + ordered[n + 1] for n in range(0, len(ordered), 2)]
            value = ordered[0]
            stride *= width
    return value


def exchange_rounds(axes):
    rounds = []
    for axis in axes:
        size = lax.axis_size(axis)
        stride = 1
        while stride < size:
            rounds.append((axis, stride, size))
            stride *= 2
    return rounds


def halving_sum(value, axes):
    shape = value.shape
    flat = value.reshape(-1)
    done = []
    for axis, stride, size in exchange_rounds(axes):
        bit = lax.axis_index(axis) // stride % 2
        halves = flat.reshape(2, -1)
        keep = lax.dynamic_index_in_dim(halves, bit, 0, keepdims=False)
        give = lax.dynamic_index_in_dim(halves, 1 - bit, 0, keepdims=False)
        pairs = [(index, index ^ stride) for index in range(size)]
        flat = keep + lax.ppermute(give, axis, pairs)
        done.append((axis, stride, size, bit))
    for axis, stride, size, bit in reversed(done):
        pairs = [(index, index ^ stride) for index in range(size)]
        other = lax.ppermute(flat, axis, pairs)
        first = jnp.where(bit == 0, flat, other)
        second = jnp.where(bit == 0, other, flat)
        flat = jnp.concatenate([first, second])
    return flat.reshape(shape)


def inverse_factors(gram_blocks):
    factors = jnp.linalg.cholesky(gram_blocks)
    identity = jnp.broadcast_to(jnp.eye(gram_blocks.shape[1], dtype=gram_blocks.dtype), gram_blocks.shape)
    return jax.scipy.linalg.solve_triangular(factors, identity, lower=True)


def shards(probe_block, prior_blocks, self_relatedness, tile_values, tile_index):
    col_count = lax.axis_size("col")
    block_count = prior_blocks.shape[0] + 1
    depth = probe_block.shape[0]
    highest = lax.Precision.HIGHEST
    basis = jnp.concatenate([prior_blocks, probe_block[None]], axis=0)
    flat_basis = basis.reshape(block_count * depth, basis.shape[2])
    wide_basis = flat_basis.astype(jnp.float32)
    gram_local = jnp.dot(flat_basis, flat_basis.T, preferred_element_type=jnp.float32)
    pairs = [(b, e) for b in range(block_count) for e in range(b + 1)]
    lower_local = jnp.stack(
        [gram_local[b * depth:(b + 1) * depth, e * depth:(e + 1) * depth] for b, e in pairs]
    )
    lower = halving_sum(lower_local, ("col", "row"))
    row_probes = lax.all_gather(probe_block, "col", axis=1, tiled=True)
    col_probes = lax.all_gather(probe_block, "row", axis=1, tiled=True)
    gram = {pair: lower[n] for n, pair in enumerate(pairs)}
    inverses = inverse_factors(jnp.stack([gram[(b, b)] for b in range(block_count)]))
    row_part, col_part = tile_products(tile_values, tile_index, row_probes, col_probes, col_count)
    row_total = sum_rows(row_part)
    col_total = sum_columns(col_part)
    product = self_relatedness[None, :] * probe_block.astype(jnp.float32) + row_total + col_total
    along_local = jnp.dot(wide_basis, product.T, precision=highest)
    along = radix_sum(along_local, ("col", "row"))
    solved = []
    for block_number in range(block_count):
        target = along[block_number * depth:(block_number + 1) * depth]
        for earlier in range(block_number):
            target = target - jnp.dot(gram[(block_number, earlier)], solved[earlier], precision=highest)
        inverse = inverses[block_number]
        half = jnp.dot(inverse, target, precision=highest)
        solved.append(jnp.dot(inverse.T, half, precision=highest))
    coefficients = jnp.concatenate(solved, axis=0)
    current = product - jnp.dot(coefficients.T, wide_basis, precision=highest)
    return (current, jnp.stack(solved))


def solution(mesh):
    in_specs = (
        P(None, ("row", "col")),
        P(None, None, ("row", "col")),
        P(("row", "col")),
        P(("row", "col"), None, None),
        P(("row", "col"), None),
    )
    out_specs = (P(None, ("row", "col")), P())
    return jax.shard_map(shards, mesh=mesh, in_specs=in_specs, out_specs=out_specs, check_vma=False)
```
